512 devices in a mesh: row: 16 (over y, core), col: 32 (over x, z).
Axes of the slice: x: 4, y: 8, z: 8, core: 2. Of those that a mesh axis runs over, the one named last changes fastest.
Arguments:
- blocks: bfloat16 [16, 64, 8, 128, 128], P('row', 'col'), may hold values from -0.375 to 0.375
- sources: int32 [16, 64, 8], P('row', 'col'), may hold values from 0 to 4
- targets: int32 [16, 64, 8], P('row', 'col'), may hold values from 0 to 4
- counts: int32 [16, 64], P('row', 'col'), may hold values from 1 to 8, as said below
- environment: bfloat16 [16, 64, 5, 128, 128], P('row', 'col'), may hold values from -6 to 6
- top_boundary: bfloat16 [64, 5, 128, 128], P('col'), may hold values from -6 to 6
- decays: float32 [16, 64, 5, 128], P('row', 'col'), may hold values from 0.3 to 1
- weights: float32 [16, 64, 5, 128, 128], P('row', 'col'), may hold values from -0.6 to 0.6
Outputs:
- grad_blocks: bfloat16 [16, 64, 8, 128, 128], P('row', 'col')
- grad_env: bfloat16 [16, 64, 5, 128, 128], P('row', 'col')
- grad_decays: float32 [16, 64, 5, 128], P('row', 'col')
The draws below stay inside these ranges and needn't reach their ends.
Inputs may be any that keep to these rules, and one draw needn't show every extreme that they name: Slots from counts on are ignored; some site has exactly 8 live slots.
All inputs are finite; a program needn't handle non-finite values.
Results may differ from the reference program's by a relative error of at most 0.0049.
Values may be sent and summed in bfloat16 or wider, within the bound.
No kernel may reach another device: no remote copies, remote signals or barrier semaphores. Data moves between devices by JAX's collectives and lax.ppermute only.
A program may use at most 64 MiB of HBM per device.

```python
import jax
import jax.numpy as jnp
from jax import lax

NS = 5
BLK = 128
CHI = 128
KMAX = 8
NR = 16
GRID_VERTICALS = 64


def draw_counts(key, part):
    first, second, third = jax.random.split(jax.random.fold_in(key, 11), 3)
    left_part = jax.random.randint(first, (NR, GRID_VERTICALS), 0, KMAX)
    right_part = jax.random.randint(second, (NR, GRID_VERTICALS), 0, KMAX)
    drawn = 1 + left_part * right_part // KMAX
    chosen = jax.random.randint(third, (), 0, NR * GRID_VERTICALS)
    places = lax.broadcasted_iota(jnp.int32, (NR, GRID_VERTICALS), 0) * GRID_VERTICALS + lax.broadcasted_iota(jnp.int32, (NR, GRID_VERTICALS), 1)
    return jnp.where(places == chosen, KMAX, drawn).astype(jnp.int32)


def draw_decays(key, part):
    stochastic_seeds = jax.random.split(jax.random.fold_in(key, 23), 5)
    complete_shape = (NR, GRID_VERTICALS, NS, BLK)
    slow_share = 0.5
    slow_mark = jax.random.uniform(stochastic_seeds[0], (1, 1, NS, BLK), jnp.float32) < slow_share
    slow_rate = jax.random.uniform(stochastic_seeds[1], complete_shape, jnp.float32, 0.2, 1.0) / GRID_VERTICALS
    fast_rate = jax.random.uniform(stochastic_seeds[2], complete_shape, jnp.float32, 1.2, 2.4) / GRID_VERTICALS
    rate_all = jnp.where(slow_mark, slow_rate, fast_rate)
    vertical_sequence = lax.broadcasted_iota(jnp.int32, complete_shape, 1)
    sudden_clusters = jax.random.randint(stochastic_seeds[3], (2,), 0, GRID_VERTICALS)
    deleted_elements = (vertical_sequence == sudden_clusters[0]) | (vertical_sequence == sudden_clusters[1])
    kept = jnp.where(deleted_elements, jax.random.uniform(stochastic_seeds[4], complete_shape, jnp.float32, 0.6, 0.8), 1.0)
    return (jnp.exp(-rate_all) * kept).astype(jnp.float32)


def set_ends(array, stream_key, low, high):
    extent = array.shape
    index_at = [jax.random.randint(jax.random.fold_in(stream_key, axis), (), 0, extent[axis]) for axis in range(len(extent))]
    array = array.at[tuple(index_at)].set(low)
    longest = extent.index(max(extent))
    index_at[longest] = (index_at[longest] + 1) % extent[longest]
    return array.at[tuple(index_at)].set(high)


def steps_of(key, shape, cuts, smallest, largest):
    gain, own = 1.0, jax.random.fold_in(key, 6)
    for position, shards_of in cuts:
        heights = jnp.exp(jax.random.uniform(jax.random.fold_in(own, position), (shards_of,), jnp.float32, smallest / len(cuts), largest / len(cuts)))
        gain = gain * jnp.repeat(heights, shape[position] // shards_of).reshape([-1 if axis == position else 1 for axis in range(len(shape))])
    return gain


def normal_values(key, extent, width, most, shards=(), kind=jnp.bfloat16):
    factor_of = steps_of(key, extent, shards, -0.22, 0.18) if shards else 1.0
    values = jax.random.normal(key, extent, jnp.float32) * width * factor_of
    return jnp.minimum(jnp.maximum(values, -most), most).astype(kind)


def setup_inputs(seed: int = 0) -> dict:
    splits = jax.random.split(jax.random.key(seed), 9)
    return {
        "blocks": normal_values(splits[0], (NR, GRID_VERTICALS, KMAX, BLK, BLK), (2 * BLK) ** -0.5, 0.375, ((0, 16), (1, 32))),
        "sources": set_ends(jax.random.randint(splits[1], (NR, GRID_VERTICALS, KMAX), 0, NS), jax.random.fold_in(splits[1], 1), 0, NS - 1).astype(jnp.int32),
        "targets": set_ends(jax.random.randint(splits[2], (NR, GRID_VERTICALS, KMAX), 0, NS), jax.random.fold_in(splits[2], 1), 0, NS - 1).astype(jnp.int32),
        "counts": draw_counts(jax.random.fold_in(splits[8], 71), 0),
        "environment": normal_values(splits[4], (NR, GRID_VERTICALS, NS, BLK, CHI), 1.0, 6.0, ((0, 16), (1, 32))),
        "top_boundary": normal_values(splits[5], (GRID_VERTICALS, NS, BLK, CHI), 1.0, 6.0, ((0, 32),)),
        "decays": draw_decays(jax.random.fold_in(splits[8], 71), 0),
        "weights": normal_values(splits[7], (NR, GRID_VERTICALS, NS, BLK, CHI), 0.1, 0.6, ((0, 16), (1, 32)), jnp.float32),
    }


def slot_tables(sources, targets, counts, sector_count):
    active_slot_list = lax.broadcasted_iota(jnp.int32, sources.shape, 1) < counts[:, None]
    sector_ids = lax.broadcasted_iota(jnp.int32, sources.shape + (sector_count,), 2)
    src_pick = sources[..., None] == sector_ids
    dst_pick = targets[..., None] == sector_ids
    return src_pick, dst_pick, active_slot_list


def forward_row(packed):
    blocks, sources, targets, counts, above_env = packed
    src_pick, dst_pick, active_slot_list = slot_tables(sources, targets, counts, above_env.shape[1])
    gathered = jnp.einsum('ckn,cnbj->ckbj', src_pick.astype(jnp.bfloat16), above_env, preferred_element_type=jnp.float32).astype(jnp.bfloat16)
    products = jnp.einsum('ckab,ckbj->ckaj', blocks, gathered, preferred_element_type=jnp.float32)
    placed = (dst_pick & active_slot_list[..., None]).astype(jnp.float32)
    return jnp.einsum('ckn,ckaj->cnaj', placed, products, precision=lax.Precision.HIGHEST)


def backward_row(packed):
    blocks, sources, targets, counts, above_env, rounded = packed
    src_pick, dst_pick, active_slot_list = slot_tables(sources, targets, counts, above_env.shape[1])
    gathered = jnp.einsum('ckn,cnbj->ckbj', src_pick.astype(jnp.bfloat16), above_env, preferred_element_type=jnp.float32).astype(jnp.bfloat16)
    picked = jnp.einsum('ckn,cnaj->ckaj', dst_pick.astype(jnp.bfloat16), rounded, preferred_element_type=jnp.float32).astype(jnp.bfloat16)
    slot_mask = active_slot_list.astype(jnp.float32)[..., None, None]
    grads = (jnp.einsum('ckaj,ckbj->ckab', picked, gathered, preferred_element_type=jnp.float32) * slot_mask).astype(jnp.bfloat16)
    contrib = jnp.einsum('ckab,ckaj->ckbj', blocks, picked, preferred_element_type=jnp.float32)
    taken = (src_pick & active_slot_list[..., None]).astype(jnp.float32)
    returned = jnp.einsum('ckn,ckbj->cnbj', taken, contrib, precision=lax.Precision.HIGHEST).astype(jnp.bfloat16)
    return grads, returned


def reference(blocks, sources, targets, counts, environment, top_boundary, decays, weights):
    above_env = jnp.concatenate([top_boundary[None], environment[:-1]], 0)
    transferred = lax.map(forward_row, (blocks, sources, targets, counts, above_env))
    fresh = environment.astype(jnp.float32) + transferred

    def forward_step(carried, packed):
        decay_col, fresh_col = packed
        updated = decay_col[..., None] * carried + fresh_col
        return updated, updated

    start = jnp.zeros(fresh.shape[:1] + fresh.shape[2:], jnp.float32)
    _, stacked = lax.scan(forward_step, start, (jnp.swapaxes(decays, 0, 1), jnp.swapaxes(fresh, 0, 1)))
    states = jnp.swapaxes(stacked, 0, 1)

    def reverse_step(carried, packed):
        decay_col, weight_col = packed
        grad_col = weight_col + carried
        return decay_col[..., None] * grad_col, grad_col

    _, piled_derivative = lax.scan(reverse_step, start, (jnp.swapaxes(decays, 0, 1), jnp.swapaxes(weights, 0, 1)), reverse=True)
    condition_derivative = jnp.swapaxes(piled_derivative, 0, 1)
    before = jnp.concatenate([jnp.zeros_like(states[:, :1]), states[:, :-1]], 1)
    grad_decays = jnp.sum(condition_derivative * before, -1)
    rounded = condition_derivative.astype(jnp.bfloat16)
    grad_blocks, returned = lax.map(backward_row, (blocks, sources, targets, counts, above_env, rounded))
    after = jnp.concatenate([returned[1:], jnp.zeros_like(returned[:1])], 0)
    grad_env = (condition_derivative + after.astype(jnp.float32)).astype(jnp.bfloat16)
    return grad_blocks, grad_env, grad_decays
```

```python
import jax
import jax.numpy as jnp
from jax import lax
from jax.sharding import PartitionSpec as P


def scan_over(axis, passed, carried, reverse):
    count = lax.axis_size(axis)
    row_count, flat_rows, channel_count = carried.shape
    packed_rows = flat_rows // channel_count
    together = flat_rows % channel_count == 0
    window_a, window_b = passed, carried
    enter_a = jnp.ones_like(passed)
    enter_b = jnp.zeros_like(carried)
    distance = 1
    while distance < count:
        if reverse:
            pairs = [(source, source - distance) for source in range(distance, count)]
        else:
            pairs = [(source, source + distance) for source in range(count - distance)]
        if together:
            sent = jnp.concatenate(
                [window_b, window_a.reshape(row_count, packed_rows, channel_count)], 1
            )
            got = lax.ppermute(sent, axis, pairs)
            got_b = got[:, :flat_rows]
            got_a = got[:, flat_rows:].reshape(row_count, flat_rows)
        else:
            got_a, got_b = lax.ppermute((window_a, window_b), axis, pairs)
        enter_b = enter_a[..., None] * got_b + enter_b
        enter_a = enter_a * got_a
        if 2 * distance < count:
            window_b = window_a[..., None] * got_b + window_b
            window_a = window_a * got_a
        distance *= 2
    return enter_b


def from_behind(value, axis, steps):
    count = lax.axis_size(axis)
    initial, last = (max(0, -steps), min(count, count - steps))
    return lax.ppermute(value, axis, [(source, source + steps) for source in range(initial, last)])


def slot_tables(sources, targets, counts, sector_count):
    active_slot_list = lax.broadcasted_iota(jnp.int32, sources.shape, 2) < counts[:, :, None]
    sector_ids = lax.broadcasted_iota(jnp.int32, sources.shape + (sector_count,), 3)
    src_pick = sources[..., None] == sector_ids
    dst_pick = targets[..., None] == sector_ids
    return (src_pick, dst_pick, active_slot_list)


def forward_blocks(blocks, above_env, src_pick, dst_pick, active_slot_list):
    placed = (dst_pick & active_slot_list[..., None]).astype(jnp.float32)
    src_bf = src_pick.astype(jnp.bfloat16)
    gathered = jnp.einsum(
        "rckn,rcnbj->rckbj", src_bf, above_env, preferred_element_type=jnp.float32
    ).astype(jnp.bfloat16)
    products = jnp.einsum(
        "rckab,rckbj->rckaj", blocks, gathered, preferred_element_type=jnp.float32
    )
    return jnp.einsum("rckn,rckaj->rcnaj", placed, products, precision=lax.Precision.HIGHEST)


def backward_blocks(blocks, above_env, rounded, src_pick, dst_pick, active_slot_list):
    taken = (src_pick & active_slot_list[..., None]).astype(jnp.float32)
    src_bf = src_pick.astype(jnp.bfloat16)
    dst_bf = dst_pick.astype(jnp.bfloat16)
    slot_live = active_slot_list.astype(jnp.float32)
    gathered = jnp.einsum(
        "rckn,rcnbj->rckbj", src_bf, above_env, preferred_element_type=jnp.float32
    ).astype(jnp.bfloat16)
    picked = jnp.einsum(
        "rckn,rcnaj->rckaj", dst_bf, rounded, preferred_element_type=jnp.float32
    ).astype(jnp.bfloat16)
    grads = (
        jnp.einsum("rckaj,rckbj->rckab", picked, gathered, preferred_element_type=jnp.float32)
        * slot_live[..., None, None]
    ).astype(jnp.bfloat16)
    contrib = jnp.einsum("rckab,rckaj->rckbj", blocks, picked, preferred_element_type=jnp.float32)
    returned = jnp.einsum(
        "rckn,rckbj->rcnbj", taken, contrib, precision=lax.Precision.HIGHEST
    ).astype(jnp.bfloat16)
    return (grads, returned)


def chain_scan(fresh, decay_rows, cotangent):
    row_count, col_count, flat_rows, channel_count = fresh.shape
    identity = (
        jnp.ones((row_count, flat_rows), jnp.float32),
        jnp.zeros((row_count, flat_rows, channel_count), jnp.float32),
    )
    states_now = identity[1]
    passed = identity[0]
    local_states = []
    reach_decay = []
    for column in range(col_count):
        states_now = decay_rows[:, column, :, None] * states_now + fresh[:, column]
        passed = passed * decay_rows[:, column]
        local_states.append(states_now)
        reach_decay.append(passed)
    entering = scan_over("col", passed, states_now, False)
    full_states = [
        local_states[column] + reach_decay[column][..., None] * entering
        for column in range(col_count)
    ]
    before_states = [entering] + full_states[:-1]
    carried = identity[1]
    tail_decay = identity[0]
    local_grads = [None] * col_count
    tail_list = [None] * col_count
    for column in reversed(range(col_count)):
        local_grads[column] = cotangent[:, column] + carried
        tail_list[column] = tail_decay
        carried = decay_rows[:, column, :, None] * local_grads[column]
        tail_decay = tail_decay * decay_rows[:, column]
    arriving = scan_over("col", tail_decay, carried, True)
    full_grads = [
        local_grads[column] + tail_list[column][..., None] * arriving
        for column in range(col_count)
    ]
    condition_derivative = jnp.stack(full_grads, 1)
    gate_grad = jnp.stack(
        [jnp.sum(full_grads[column] * before_states[column], -1) for column in range(col_count)], 1
    )
    return (condition_derivative, gate_grad)


def local(blocks, sources, targets, counts, environment, top_boundary, decays, weights):
    row_count, col_count, sector_count, block_rows, channel_count = environment.shape
    flat_rows = sector_count * block_rows
    bottom = environment[row_count - 1]
    upper_env = from_behind(bottom, "row", 1)
    upper_env = jnp.where(lax.axis_index("row") == 0, top_boundary, upper_env)
    above_env = jnp.concatenate([upper_env[None], environment[: row_count - 1]], 0)
    src_pick, dst_pick, active_slot_list = slot_tables(sources, targets, counts, sector_count)
    transferred = forward_blocks(blocks, above_env, src_pick, dst_pick, active_slot_list)
    fresh = (environment.astype(jnp.float32) + transferred).reshape(
        row_count, col_count, flat_rows, channel_count
    )
    decay_rows = decays.reshape(row_count, col_count, flat_rows)
    cotangent = weights.reshape(row_count, col_count, flat_rows, channel_count)
    condition_derivative, gate_grad = chain_scan(fresh, decay_rows, cotangent)
    condition_derivative = condition_derivative.reshape(environment.shape)
    rounded = condition_derivative.astype(jnp.bfloat16)
    grad_blocks, returned = backward_blocks(
        blocks, above_env, rounded, src_pick, dst_pick, active_slot_list
    )
    below_rows = from_behind(returned[0], "row", -1)
    following_horizontals = jnp.concatenate([returned[1:], below_rows[None]], 0)
    grad_env = (condition_derivative + following_horizontals.astype(jnp.float32)).astype(
        jnp.bfloat16
    )
    grad_decays = gate_grad.reshape(decays.shape)
    return (grad_blocks, grad_env, grad_decays)


def solution(mesh):
    in_specs = (
        P("row", "col", None, None, None),
        P("row", "col", None),
        P("row", "col", None),
        P("row", "col"),
        P("row", "col", None, None, None),
        P("col", None, None, None),
        P("row", "col", None, None),
        P("row", "col", None, None, None),
    )
    out_specs = (
        P("row", "col", None, None, None),
        P("row", "col", None, None, None),
        P("row", "col", None, None),
    )
    return jax.shard_map(local, mesh=mesh, in_specs=in_specs, out_specs=out_specs, check_vma=False)
```

```python
import jax
import jax.numpy as jnp
from jax import lax
from jax.sharding import PartitionSpec as P
from jax.experimental import pallas as pl
from jax.experimental.pallas import tpu as pltpu


def from_behind(value, axis, steps):
    count = lax.axis_size(axis)
    initial, last = (max(0, -steps), min(count, count - steps))
    return lax.ppermute(value, axis, [(source, source + steps) for source in range(initial, last)])


def slot_tables(sources, targets, counts, sector_count):
    active_slot_list = lax.broadcasted_iota(jnp.int32, sources.shape, 2) < counts[:, :, None]
    sector_ids = lax.broadcasted_iota(jnp.int32, sources.shape + (sector_count,), 3)
    src_pick = sources[..., None] == sector_ids
    dst_pick = targets[..., None] == sector_ids
    return (src_pick, dst_pick, active_slot_list)


def forward_blocks(blocks, above_env, src_pick, dst_pick, active_slot_list):
    placed = (dst_pick & active_slot_list[..., None]).astype(jnp.float32)
    src_bf = src_pick.astype(jnp.bfloat16)
    gathered = jnp.einsum(
        "rckn,rcnbj->rckbj", src_bf, above_env, preferred_element_type=jnp.float32
    ).astype(jnp.bfloat16)
    products = jnp.einsum(
        "rckab,rckbj->rckaj", blocks, gathered, preferred_element_type=jnp.float32
    )
    return jnp.einsum("rckn,rckaj->rcnaj", placed, products, precision=lax.Precision.HIGHEST)


def backward_blocks(blocks, above_env, rounded, src_pick, dst_pick, active_slot_list):
    taken = (src_pick & active_slot_list[..., None]).astype(jnp.float32)
    src_bf = src_pick.astype(jnp.bfloat16)
    dst_bf = dst_pick.astype(jnp.bfloat16)
    slot_live = active_slot_list.astype(jnp.float32)
    gathered = jnp.einsum(
        "rckn,rcnbj->rckbj", src_bf, above_env, preferred_element_type=jnp.float32
    ).astype(jnp.bfloat16)
    picked = jnp.einsum(
        "rckn,rcnaj->rckaj", dst_bf, rounded, preferred_element_type=jnp.float32
    ).astype(jnp.bfloat16)
    grads = (
        jnp.einsum("rckaj,rckbj->rckab", picked, gathered, preferred_element_type=jnp.float32)
        * slot_live[..., None, None]
    ).astype(jnp.bfloat16)
    contrib = jnp.einsum("rckab,rckaj->rckbj", blocks, picked, preferred_element_type=jnp.float32)
    returned = jnp.einsum(
        "rckn,rckbj->rcnbj", taken, contrib, precision=lax.Precision.HIGHEST
    ).astype(jnp.bfloat16)
    return (grads, returned)


def recurrence_kernel(fresh_t, weights_t, decays_t):
    col_total, part, channel_count = fresh_t.shape

    def body(fresh_ref, weight_ref, decay_ref, grad_ref, gate_ref, state_ref):
        state = jnp.zeros((part, channel_count), jnp.float32)
        for column in range(col_total):
            state = decay_ref[column] * state + fresh_ref[column]
            state_ref[column] = state
        carried = jnp.zeros((part, channel_count), jnp.float32)
        for column in reversed(range(col_total)):
            grad = weight_ref[column] + carried
            grad_ref[column] = grad
            if column > 0:
                gate_ref[column] = jnp.sum(grad * state_ref[column - 1], axis=-1, keepdims=True)
            else:
                gate_ref[column] = jnp.zeros((part, 1), jnp.float32)
            carried = decay_ref[column] * grad

    return pl.pallas_call(
        body,
        out_shape=(
            jax.ShapeDtypeStruct((col_total, part, channel_count), jnp.float32),
            jax.ShapeDtypeStruct((col_total, part, 1), jnp.float32),
        ),
        scratch_shapes=[pltpu.VMEM((col_total, part, channel_count), jnp.float32)],
    )(fresh_t, weights_t, decays_t)


def chain_scan(fresh, decay_rows, cotangent):
    row_count, col_count, flat_rows, channel_count = fresh.shape
    count = lax.axis_size("col")
    rows = row_count * flat_rows
    part = rows // count
    assert part * count == rows and part <= channel_count
    col_total = count * col_count

    def by_column(value):
        return jnp.swapaxes(value, 0, 1).reshape(col_count, count, part, -1)

    decay_lane = jnp.pad(
        by_column(decay_rows).reshape(col_count, count, 1, part),
        ((0, 0), (0, 0), (0, 0), (0, channel_count - part)),
    )
    payload = jnp.concatenate([by_column(fresh), by_column(cotangent), decay_lane], 2)
    payload = jnp.swapaxes(payload, 0, 1)
    got = lax.all_to_all(payload, "col", 0, 0, tiled=True)
    got = got.reshape(col_total, 2 * part + 1, channel_count)
    grad_t, gate_t = recurrence_kernel(
        got[:, :part], got[:, part : 2 * part], got[:, 2 * part, :part][..., None]
    )
    gate_lane = jnp.pad(
        gate_t.reshape(col_total, 1, part), ((0, 0), (0, 0), (0, channel_count - part))
    )
    back = jnp.concatenate([grad_t, gate_lane], 1).reshape(count, col_count, part + 1, channel_count)
    ret = lax.all_to_all(back, "col", 0, 0, tiled=True)
    grads = jnp.swapaxes(ret[:, :, :part], 0, 1).reshape(col_count, row_count, flat_rows, channel_count)
    gates = jnp.swapaxes(ret[:, :, part, :part], 0, 1).reshape(col_count, row_count, flat_rows)
    return (jnp.swapaxes(grads, 0, 1), jnp.swapaxes(gates, 0, 1))


def local(blocks, sources, targets, counts, environment, top_boundary, decays, weights):
    row_count, col_count, sector_count, block_rows, channel_count = environment.shape
    flat_rows = sector_count * block_rows
    bottom = environment[row_count - 1]
    upper_env = from_behind(bottom, "row", 1)
    upper_env = jnp.where(lax.axis_index("row") == 0, top_boundary, upper_env)
    above_env = jnp.concatenate([upper_env[None], environment[: row_count - 1]], 0)
    src_pick, dst_pick, active_slot_list = slot_tables(sources, targets, counts, sector_count)
    transferred = forward_blocks(blocks, above_env, src_pick, dst_pick, active_slot_list)
    fresh = (environment.astype(jnp.float32) + transferred).reshape(
        row_count, col_count, flat_rows, channel_count
    )
    decay_rows = decays.reshape(row_count, col_count, flat_rows)
    cotangent = weights.reshape(row_count, col_count, flat_rows, channel_count)
    condition_derivative, gate_grad = chain_scan(fresh, decay_rows, cotangent)
    condition_derivative = condition_derivative.reshape(environment.shape)
    rounded = condition_derivative.astype(jnp.bfloat16)
    grad_blocks, returned = backward_blocks(
        blocks, above_env, rounded, src_pick, dst_pick, active_slot_list
    )
    below_rows = from_behind(returned[0], "row", -1)
    following_horizontals = jnp.concatenate([returned[1:], below_rows[None]], 0)
    grad_env = (condition_derivative + following_horizontals.astype(jnp.float32)).astype(
        jnp.bfloat16
    )
    grad_decays = gate_grad.reshape(decays.shape)
    return (grad_blocks, grad_env, grad_decays)


def solution(mesh):
    in_specs = (
        P("row", "col", None, None, None),
        P("row", "col", None),
        P("row", "col", None),
        P("row", "col"),
        P("row", "col", None, None, None),
        P("col", None, None, None),
        P("row", "col", None, None),
        P("row", "col", None, None, None),
    )
    out_specs = (
        P("row", "col", None, None, None),
        P("row", "col", None, None, None),
        P("row", "col", None, None),
    )
    return jax.shard_map(local, mesh=mesh, in_specs=in_specs, out_specs=out_specs, check_vma=False)
```

```python
import jax
import jax.numpy as jnp
from jax import lax
from jax.sharding import PartitionSpec as P
from jax.experimental import pallas as pl
from jax.experimental.pallas import tpu as pltpu


def from_behind(value, axis, steps):
    count = lax.axis_size(axis)
    initial, last = (max(0, -steps), min(count, count - steps))
    return lax.ppermute(value, axis, [(source, source + steps) for source in range(initial, last)])


def slot_tables(sources, targets, counts, sector_count):
    active_slot_list = lax.broadcasted_iota(jnp.int32, sources.shape, 2) < counts[:, :, None]
    sector_ids = lax.broadcasted_iota(jnp.int32, sources.shape + (sector_count,), 3)
    src_pick = sources[..., None] == sector_ids
    dst_pick = targets[..., None] == sector_ids
    return (src_pick, dst_pick, active_slot_list)


def forward_blocks(blocks, above_env, src_pick, dst_pick, active_slot_list):
    placed = (dst_pick & active_slot_list[..., None]).astype(jnp.float32)
    src_bf = src_pick.astype(jnp.bfloat16)
    gathered = jnp.einsum(
        "rckn,rcnbj->rckbj", src_bf, above_env, preferred_element_type=jnp.float32
    ).astype(jnp.bfloat16)
    products = jnp.einsum(
        "rckab,rckbj->rckaj", blocks, gathered, preferred_element_type=jnp.float32
    )
    return jnp.einsum("rckn,rckaj->rcnaj", placed, products, precision=lax.Precision.HIGHEST)


def backward_blocks(blocks, above_env, rounded, src_pick, dst_pick, active_slot_list):
    taken = (src_pick & active_slot_list[..., None]).astype(jnp.float32)
    src_bf = src_pick.astype(jnp.bfloat16)
    dst_bf = dst_pick.astype(jnp.bfloat16)
    slot_live = active_slot_list.astype(jnp.float32)
    gathered = jnp.einsum(
        "rckn,rcnbj->rckbj", src_bf, above_env, preferred_element_type=jnp.float32
    ).astype(jnp.bfloat16)
    picked = jnp.einsum(
        "rckn,rcnaj->rckaj", dst_bf, rounded, preferred_element_type=jnp.float32
    ).astype(jnp.bfloat16)
    grads = (
        jnp.einsum("rckaj,rckbj->rckab", picked, gathered, preferred_element_type=jnp.float32)
        * slot_live[..., None, None]
    ).astype(jnp.bfloat16)
    contrib = jnp.einsum("rckab,rckaj->rckbj", blocks, picked, preferred_element_type=jnp.float32)
    returned = jnp.einsum(
        "rckn,rckbj->rcnbj", taken, contrib, precision=lax.Precision.HIGHEST
    ).astype(jnp.bfloat16)
    return (grads, returned)


def carry_kernel(fwd_b, bwd_b, fwd_a, bwd_a):
    count, part, channel_count = fwd_b.shape

    def body(fwd_b_ref, bwd_b_ref, fwd_a_ref, bwd_a_ref, out_ref):
        state = jnp.zeros((part, channel_count), jnp.float32)
        for source in range(count):
            out_ref[source, 0] = state
            state = fwd_a_ref[source] * state + fwd_b_ref[source]
        state = jnp.zeros((part, channel_count), jnp.float32)
        for source in reversed(range(count)):
            out_ref[source, 1] = state
            state = bwd_a_ref[source] * state + bwd_b_ref[source]

    return pl.pallas_call(
        body,
        out_shape=jax.ShapeDtypeStruct((count, 2, part, channel_count), jnp.float32),
    )(fwd_b, bwd_b, fwd_a, bwd_a)


def carry_exchange(fwd_a, fwd_b, bwd_a, bwd_b):
    row_count, flat_rows, channel_count = fwd_b.shape
    count = lax.axis_size("col")
    rows = row_count * flat_rows
    part = rows // count
    assert part * count == rows and 2 * part <= channel_count
    factors = jnp.concatenate(
        [fwd_a.reshape(count, 1, part), bwd_a.reshape(count, 1, part)], 2
    )
    factors = jnp.pad(factors, ((0, 0), (0, 0), (0, channel_count - 2 * part)))
    payload = jnp.concatenate(
        [fwd_b.reshape(count, part, channel_count), bwd_b.reshape(count, part, channel_count), factors], 1
    )
    got = lax.all_to_all(payload, "col", 0, 0, tiled=True)
    carries = carry_kernel(
        got[:, :part],
        got[:, part : 2 * part],
        got[:, 2 * part, :part][..., None],
        got[:, 2 * part, part : 2 * part][..., None],
    )
    ret = lax.all_to_all(carries, "col", 0, 0, tiled=True)
    entering = ret[:, 0].reshape(row_count, flat_rows, channel_count)
    arriving = ret[:, 1].reshape(row_count, flat_rows, channel_count)
    return (entering, arriving)


def chain_scan(fresh, decay_rows, cotangent):
    row_count, col_count, flat_rows, channel_count = fresh.shape
    identity = (
        jnp.ones((row_count, flat_rows), jnp.float32),
        jnp.zeros((row_count, flat_rows, channel_count), jnp.float32),
    )
    states_now = identity[1]
    passed = identity[0]
    local_states = []
    reach_decay = []
    for column in range(col_count):
        states_now = decay_rows[:, column, :, None] * states_now + fresh[:, column]
        passed = passed * decay_rows[:, column]
        local_states.append(states_now)
        reach_decay.append(passed)
    carried = identity[1]
    tail_decay = identity[0]
    local_grads = [None] * col_count
    tail_list = [None] * col_count
    for column in reversed(range(col_count)):
        local_grads[column] = cotangent[:, column] + carried
        tail_list[column] = tail_decay
        carried = decay_rows[:, column, :, None] * local_grads[column]
        tail_decay = tail_decay * decay_rows[:, column]
    entering, arriving = carry_exchange(passed, states_now, tail_decay, carried)
    full_states = [
        local_states[column] + reach_decay[column][..., None] * entering
        for column in range(col_count)
    ]
    before_states = [entering] + full_states[:-1]
    full_grads = [
        local_grads[column] + tail_list[column][..., None] * arriving
        for column in range(col_count)
    ]
    condition_derivative = jnp.stack(full_grads, 1)
    gate_grad = jnp.stack(
        [jnp.sum(full_grads[column] * before_states[column], -1) for column in range(col_count)], 1
    )
    return (condition_derivative, gate_grad)


def local(blocks, sources, targets, counts, environment, top_boundary, decays, weights):
    row_count, col_count, sector_count, block_rows, channel_count = environment.shape
    flat_rows = sector_count * block_rows
    bottom = environment[row_count - 1]
    upper_env = from_behind(bottom, "row", 1)
    upper_env = jnp.where(lax.axis_index("row") == 0, top_boundary, upper_env)
    above_env = jnp.concatenate([upper_env[None], environment[: row_count - 1]], 0)
    src_pick, dst_pick, active_slot_list = slot_tables(sources, targets, counts, sector_count)
    transferred = forward_blocks(blocks, above_env, src_pick, dst_pick, active_slot_list)
    fresh = (environment.astype(jnp.float32) + transferred).reshape(
        row_count, col_count, flat_rows, channel_count
    )
    decay_rows = decays.reshape(row_count, col_count, flat_rows)
    cotangent = weights.reshape(row_count, col_count, flat_rows, channel_count)
    condition_derivative, gate_grad = chain_scan(fresh, decay_rows, cotangent)
    condition_derivative = condition_derivative.reshape(environment.shape)
    rounded = condition_derivative.astype(jnp.bfloat16)
    grad_blocks, returned = backward_blocks(
        blocks, above_env, rounded, src_pick, dst_pick, active_slot_list
    )
    below_rows = from_behind(returned[0], "row", -1)
    following_horizontals = jnp.concatenate([returned[1:], below_rows[None]], 0)
    grad_env = (condition_derivative + following_horizontals.astype(jnp.float32)).astype(
        jnp.bfloat16
    )
    grad_decays = gate_grad.reshape(decays.shape)
    return (grad_blocks, grad_env, grad_decays)


def solution(mesh):
    in_specs = (
        P("row", "col", None, None, None),
        P("row", "col", None),
        P("row", "col", None),
        P("row", "col"),
        P("row", "col", None, None, None),
        P("col", None, None, None),
        P("row", "col", None, None),
        P("row", "col", None, None, None),
    )
    out_specs = (
        P("row", "col", None, None, None),
        P("row", "col", None, None, None),
        P("row", "col", None, None),
    )
    return jax.shard_map(local, mesh=mesh, in_specs=in_specs, out_specs=out_specs, check_vma=False)
```

```python
import jax
import jax.numpy as jnp
from jax import lax
from jax.sharding import PartitionSpec as P
from jax.experimental import pallas as pl
from jax.experimental.pallas import tpu as pltpu


def from_behind(value, axis, steps):
    count = lax.axis_size(axis)
    initial, last = (max(0, -steps), min(count, count - steps))
    return lax.ppermute(value, axis, [(source, source + steps) for source in range(initial, last)])


def slot_tables(sources, targets, counts, sector_count):
    active_slot_list = lax.broadcasted_iota(jnp.int32, sources.shape, 2) < counts[:, :, None]
    sector_ids = lax.broadcasted_iota(jnp.int32, sources.shape + (sector_count,), 3)
    src_pick = sources[..., None] == sector_ids
    dst_pick = targets[..., None] == sector_ids
    return (src_pick, dst_pick, active_slot_list)


def forward_blocks(blocks, above_env, src_pick, dst_pick, active_slot_list):
    placed = (dst_pick & active_slot_list[..., None]).astype(jnp.float32)
    src_bf = src_pick.astype(jnp.bfloat16)
    gathered = jnp.einsum(
        "rckn,rcnbj->rckbj", src_bf, above_env, preferred_element_type=jnp.float32
    ).astype(jnp.bfloat16)
    products = jnp.einsum(
        "rckab,rckbj->rckaj", blocks, gathered, preferred_element_type=jnp.float32
    )
    return jnp.einsum("rckn,rckaj->rcnaj", placed, products, precision=lax.Precision.HIGHEST)


def backward_blocks(blocks, above_env, rounded, src_pick, dst_pick, active_slot_list):
    taken = (src_pick & active_slot_list[..., None]).astype(jnp.float32)
    src_bf = src_pick.astype(jnp.bfloat16)
    dst_bf = dst_pick.astype(jnp.bfloat16)
    slot_live = active_slot_list.astype(jnp.float32)
    gathered = jnp.einsum(
        "rckn,rcnbj->rckbj", src_bf, above_env, preferred_element_type=jnp.float32
    ).astype(jnp.bfloat16)
    picked = jnp.einsum(
        "rckn,rcnaj->rckaj", dst_bf, rounded, preferred_element_type=jnp.float32
    ).astype(jnp.bfloat16)
    grads = (
        jnp.einsum("rckaj,rckbj->rckab", picked, gathered, preferred_element_type=jnp.float32)
        * slot_live[..., None, None]
    ).astype(jnp.bfloat16)
    contrib = jnp.einsum("rckab,rckaj->rckbj", blocks, picked, preferred_element_type=jnp.float32)
    returned = jnp.einsum(
        "rckn,rckbj->rcnbj", taken, contrib, precision=lax.Precision.HIGHEST
    ).astype(jnp.bfloat16)
    return (grads, returned)


def carry_kernel(fwd_b, bwd_b, factor):
    count, part, channel_count = fwd_b.shape

    def body(fwd_b_ref, bwd_b_ref, factor_ref, out_ref):
        state = jnp.zeros((part, channel_count), jnp.float32)
        for source in range(count):
            out_ref[source, 0] = state
            state = factor_ref[source] * state + fwd_b_ref[source]
        state = jnp.zeros((part, channel_count), jnp.float32)
        for source in reversed(range(count)):
            out_ref[source, 1] = state
            state = factor_ref[source] * state + bwd_b_ref[source]

    return pl.pallas_call(
        body,
        out_shape=jax.ShapeDtypeStruct((count, 2, part, channel_count), jnp.float32),
    )(fwd_b, bwd_b, factor)


def summary_kernel(fresh, cotangent, decay_col, factor_row, count):
    col_count, rows, channel_count = fresh.shape
    part = rows // count

    def body(fresh_ref, weight_ref, decay_ref, factor_ref, out_ref):
        for chunk in range(count):
            span = pl.ds(chunk * part, part)
            state = fresh_ref[0, span, :]
            for column in range(1, col_count):
                state = decay_ref[column, span, :] * state + fresh_ref[column, span, :]
            grad = weight_ref[col_count - 1, span, :]
            for column in reversed(range(col_count - 1)):
                grad = weight_ref[column, span, :] + decay_ref[column + 1, span, :] * grad
            grad = decay_ref[0, span, :] * grad
            out_ref[chunk, pl.ds(0, part), :] = state
            out_ref[chunk, pl.ds(part, part), :] = grad
            out_ref[chunk, pl.ds(2 * part, 1), :] = factor_ref[pl.ds(chunk, 1), :]

    return pl.pallas_call(
        body,
        out_shape=jax.ShapeDtypeStruct((count, 2 * part + 1, channel_count), jnp.float32),
    )(fresh, cotangent, decay_col, factor_row)


def fixup_kernel(fresh, cotangent, decay_col, carries):
    col_count, rows, channel_count = fresh.shape
    count, _, part, _ = carries.shape

    def body(fresh_ref, weight_ref, decay_ref, carry_ref, grad_ref, gate_ref):
        for chunk in range(count):
            span = pl.ds(chunk * part, part)
            grad = carry_ref[chunk, 1]
            grads = [None] * col_count
            for column in reversed(range(col_count)):
                grad = weight_ref[column, span, :] + grad
                grads[column] = grad
                grad_ref[column, span, :] = grad
                grad = decay_ref[column, span, :] * grad
            state = carry_ref[chunk, 0]
            for column in range(col_count):
                gate_ref[column, span, :] = jnp.sum(grads[column] * state, axis=-1, keepdims=True)
                state = decay_ref[column, span, :] * state + fresh_ref[column, span, :]

    return pl.pallas_call(
        body,
        out_shape=(
            jax.ShapeDtypeStruct((col_count, rows, channel_count), jnp.float32),
            jax.ShapeDtypeStruct((col_count, rows, 1), jnp.float32),
        ),
    )(fresh, cotangent, decay_col, carries)


def chain_scan(fresh, decay_rows, cotangent):
    row_count, col_count, flat_rows, channel_count = fresh.shape
    count = lax.axis_size("col")
    rows = row_count * flat_rows
    part = rows // count
    assert part * count == rows and part <= channel_count

    def by_column(value):
        return jnp.swapaxes(value, 0, 1).reshape(col_count, rows, -1)

    fresh_c = by_column(fresh)
    weight_c = by_column(cotangent)
    decay_c = by_column(decay_rows[..., None])
    factor = jnp.prod(jnp.swapaxes(decay_rows, 0, 1).reshape(col_count, count, part), 0)
    factor_row = jnp.pad(factor, ((0, 0), (0, channel_count - part)))
    payload = summary_kernel(fresh_c, weight_c, decay_c, factor_row, count)
    got = lax.all_to_all(payload, "col", 0, 0, tiled=True)
    carries = carry_kernel(got[:, :part], got[:, part : 2 * part], got[:, 2 * part, :part][..., None])
    ret = lax.all_to_all(carries, "col", 0, 0, tiled=True)
    grads, gates = fixup_kernel(fresh_c, weight_c, decay_c, ret)
    grads = jnp.swapaxes(grads.reshape(col_count, row_count, flat_rows, channel_count), 0, 1)
    gates = jnp.swapaxes(gates.reshape(col_count, row_count, flat_rows), 0, 1)
    return (grads, gates)


def local(blocks, sources, targets, counts, environment, top_boundary, decays, weights):
    row_count, col_count, sector_count, block_rows, channel_count = environment.shape
    flat_rows = sector_count * block_rows
    bottom = environment[row_count - 1]
    upper_env = from_behind(bottom, "row", 1)
    upper_env = jnp.where(lax.axis_index("row") == 0, top_boundary, upper_env)
    above_env = jnp.concatenate([upper_env[None], environment[: row_count - 1]], 0)
    src_pick, dst_pick, active_slot_list = slot_tables(sources, targets, counts, sector_count)
    transferred = forward_blocks(blocks, above_env, src_pick, dst_pick, active_slot_list)
    fresh = (environment.astype(jnp.float32) + transferred).reshape(
        row_count, col_count, flat_rows, channel_count
    )
    decay_rows = decays.reshape(row_count, col_count, flat_rows)
    cotangent = weights.reshape(row_count, col_count, flat_rows, channel_count)
    condition_derivative, gate_grad = chain_scan(fresh, decay_rows, cotangent)
    condition_derivative = condition_derivative.reshape(environment.shape)
    rounded = condition_derivative.astype(jnp.bfloat16)
    grad_blocks, returned = backward_blocks(
        blocks, above_env, rounded, src_pick, dst_pick, active_slot_list
    )
    below_rows = from_behind(returned[0], "row", -1)
    following_horizontals = jnp.concatenate([returned[1:], below_rows[None]], 0)
    grad_env = (condition_derivative + following_horizontals.astype(jnp.float32)).astype(
        jnp.bfloat16
    )
    grad_decays = gate_grad.reshape(decays.shape)
    return (grad_blocks, grad_env, grad_decays)


def solution(mesh):
    in_specs = (
        P("row", "col", None, None, None),
        P("row", "col", None),
        P("row", "col", None),
        P("row", "col"),
        P("row", "col", None, None, None),
        P("col", None, None, None),
        P("row", "col", None, None),
        P("row", "col", None, None, None),
    )
    out_specs = (
        P("row", "col", None, None, None),
        P("row", "col", None, None, None),
        P("row", "col", None, None),
    )
    return jax.shard_map(local, mesh=mesh, in_specs=in_specs, out_specs=out_specs, check_vma=False)
```

```python
import jax
import jax.numpy as jnp
from jax import lax
from jax.sharding import PartitionSpec as P
from jax.experimental import pallas as pl
from jax.experimental.pallas import tpu as pltpu


def from_behind(value, axis, steps):
    count = lax.axis_size(axis)
    initial, last = (max(0, -steps), min(count, count - steps))
    return lax.ppermute(value, axis, [(source, source + steps) for source in range(initial, last)])


def slot_tables(sources, targets, counts, sector_count):
    active_slot_list = lax.broadcasted_iota(jnp.int32, sources.shape, 2) < counts[:, :, None]
    sector_ids = lax.broadcasted_iota(jnp.int32, sources.shape + (sector_count,), 3)
    src_pick = sources[..., None] == sector_ids
    dst_pick = targets[..., None] == sector_ids
    return (src_pick, dst_pick, active_slot_list)


def forward_blocks(blocks, above_env, src_pick, dst_pick, active_slot_list):
    placed = (dst_pick & active_slot_list[..., None]).astype(jnp.float32)
    src_bf = src_pick.astype(jnp.bfloat16)
    gathered = jnp.einsum(
        "rckn,rcnbj->rckbj", src_bf, above_env, preferred_element_type=jnp.float32
    ).astype(jnp.bfloat16)
    products = jnp.einsum(
        "rckab,rckbj->rckaj", blocks, gathered, preferred_element_type=jnp.float32
    )
    return jnp.einsum("rckn,rckaj->rcnaj", placed, products, precision=lax.Precision.HIGHEST)


def backward_blocks(blocks, above_env, rounded, src_pick, dst_pick, active_slot_list):
    taken = (src_pick & active_slot_list[..., None]).astype(jnp.float32)
    src_bf = src_pick.astype(jnp.bfloat16)
    dst_bf = dst_pick.astype(jnp.bfloat16)
    slot_live = active_slot_list.astype(jnp.float32)
    gathered = jnp.einsum(
        "rckn,rcnbj->rckbj", src_bf, above_env, preferred_element_type=jnp.float32
    ).astype(jnp.bfloat16)
    picked = jnp.einsum(
        "rckn,rcnaj->rckaj", dst_bf, rounded, preferred_element_type=jnp.float32
    ).astype(jnp.bfloat16)
    grads = (
        jnp.einsum("rckaj,rckbj->rckab", picked, gathered, preferred_element_type=jnp.float32)
        * slot_live[..., None, None]
    ).astype(jnp.bfloat16)
    contrib = jnp.einsum("rckab,rckaj->rckbj", blocks, picked, preferred_element_type=jnp.float32)
    returned = jnp.einsum(
        "rckn,rckbj->rcnbj", taken, contrib, precision=lax.Precision.HIGHEST
    ).astype(jnp.bfloat16)
    return (grads, returned)


def carry_kernel(fwd_b, bwd_b, factor):
    count, part, channel_count = fwd_b.shape

    def body(fwd_b_ref, bwd_b_ref, factor_ref, out_ref):
        state = jnp.zeros((part, channel_count), jnp.float32)
        for source in range(count):
            out_ref[source, 0] = state
            state = factor_ref[source] * state + fwd_b_ref[source]
        state = jnp.zeros((part, channel_count), jnp.float32)
        for source in reversed(range(count)):
            out_ref[source, 1] = state
            state = factor_ref[source] * state + bwd_b_ref[source]

    return pl.pallas_call(
        body,
        out_shape=jax.ShapeDtypeStruct((count, 2, part, channel_count), jnp.float32),
    )(fwd_b, bwd_b, factor)


def summary_kernel(fresh, cotangent, decay_col, factor_row, count):
    col_count, rows, channel_count = fresh.shape
    part = rows // count

    def body(fresh_ref, weight_ref, decay_ref, factor_ref, out_ref):
        for chunk in range(count):
            span = pl.ds(chunk * part, part)
            state = fresh_ref[0, span, :]
            for column in range(1, col_count):
                state = decay_ref[column, span, :] * state + fresh_ref[column, span, :]
            grad = weight_ref[col_count - 1, span, :]
            for column in reversed(range(col_count - 1)):
                grad = weight_ref[column, span, :] + decay_ref[column + 1, span, :] * grad
            grad = decay_ref[0, span, :] * grad
            out_ref[chunk, pl.ds(0, part), :] = state
            out_ref[chunk, pl.ds(part, part), :] = grad
            out_ref[chunk, pl.ds(2 * part, 2), :] = factor_ref[chunk]

    return pl.pallas_call(
        body,
        out_shape=jax.ShapeDtypeStruct((count, 2 * part + 2, channel_count), jnp.float32),
    )(fresh, cotangent, decay_col, factor_row)


def fixup_kernel(fresh, cotangent, decay_col, carries):
    col_count, rows, channel_count = fresh.shape
    count, _, part, _ = carries.shape

    def body(fresh_ref, weight_ref, decay_ref, carry_ref, grad_ref, gate_ref):
        for chunk in range(count):
            span = pl.ds(chunk * part, part)
            grad = carry_ref[chunk, 1].astype(jnp.float32)
            grads = [None] * col_count
            for column in reversed(range(col_count)):
                grad = weight_ref[column, span, :] + grad
                grads[column] = grad
                grad_ref[column, span, :] = grad
                grad = decay_ref[column, span, :] * grad
            state = carry_ref[chunk, 0].astype(jnp.float32)
            for column in range(col_count):
                gate_ref[column, span, :] = jnp.sum(grads[column] * state, axis=-1, keepdims=True)
                state = decay_ref[column, span, :] * state + fresh_ref[column, span, :]

    return pl.pallas_call(
        body,
        out_shape=(
            jax.ShapeDtypeStruct((col_count, rows, channel_count), jnp.float32),
            jax.ShapeDtypeStruct((col_count, rows, 1), jnp.float32),
        ),
    )(fresh, cotangent, decay_col, carries)


def chain_scan(fresh, decay_rows, cotangent):
    row_count, col_count, flat_rows, channel_count = fresh.shape
    count = lax.axis_size("col")
    rows = row_count * flat_rows
    part = rows // count
    assert part * count == rows and part <= channel_count

    def by_column(value):
        return jnp.swapaxes(value, 0, 1).reshape(col_count, rows, -1)

    fresh_c = by_column(fresh)
    weight_c = by_column(cotangent)
    decay_c = by_column(decay_rows[..., None])
    factor = jnp.prod(jnp.swapaxes(decay_rows, 0, 1).reshape(col_count, count, part), 0)
    factor_high = factor.astype(jnp.bfloat16).astype(jnp.float32)
    factor_low = (factor - factor_high).astype(jnp.bfloat16).astype(jnp.float32)
    factor_row = jnp.pad(
        jnp.stack([factor_high, factor_low], 1), ((0, 0), (0, 0), (0, channel_count - part))
    )
    payload = summary_kernel(fresh_c, weight_c, decay_c, factor_row, count)
    got = lax.all_to_all(payload.astype(jnp.bfloat16), "col", 0, 0, tiled=True).astype(jnp.float32)
    factor_got = got[:, 2 * part, :part] + got[:, 2 * part + 1, :part]
    carries = carry_kernel(got[:, :part], got[:, part : 2 * part], factor_got[..., None])
    ret = lax.all_to_all(carries.astype(jnp.bfloat16), "col", 0, 0, tiled=True)
    grads, gates = fixup_kernel(fresh_c, weight_c, decay_c, ret)
    grads = jnp.swapaxes(grads.reshape(col_count, row_count, flat_rows, channel_count), 0, 1)
    gates = jnp.swapaxes(gates.reshape(col_count, row_count, flat_rows), 0, 1)
    return (grads, gates)


def local(blocks, sources, targets, counts, environment, top_boundary, decays, weights):
    row_count, col_count, sector_count, block_rows, channel_count = environment.shape
    flat_rows = sector_count * block_rows
    bottom = environment[row_count - 1]
    upper_env = from_behind(bottom, "row", 1)
    upper_env = jnp.where(lax.axis_index("row") == 0, top_boundary, upper_env)
    above_env = jnp.concatenate([upper_env[None], environment[: row_count - 1]], 0)
    src_pick, dst_pick, active_slot_list = slot_tables(sources, targets, counts, sector_count)
    transferred = forward_blocks(blocks, above_env, src_pick, dst_pick, active_slot_list)
    fresh = (environment.astype(jnp.float32) + transferred).reshape(
        row_count, col_count, flat_rows, channel_count
    )
    decay_rows = decays.reshape(row_count, col_count, flat_rows)
    cotangent = weights.reshape(row_count, col_count, flat_rows, channel_count)
    condition_derivative, gate_grad = chain_scan(fresh, decay_rows, cotangent)
    condition_derivative = condition_derivative.reshape(environment.shape)
    rounded = condition_derivative.astype(jnp.bfloat16)
    grad_blocks, returned = backward_blocks(
        blocks, above_env, rounded, src_pick, dst_pick, active_slot_list
    )
    below_rows = from_behind(returned[0], "row", -1)
    following_horizontals = jnp.concatenate([returned[1:], below_rows[None]], 0)
    grad_env = (condition_derivative + following_horizontals.astype(jnp.float32)).astype(
        jnp.bfloat16
    )
    grad_decays = gate_grad.reshape(decays.shape)
    return (grad_blocks, grad_env, grad_decays)


def solution(mesh):
    in_specs = (
        P("row", "col", None, None, None),
        P("row", "col", None),
        P("row", "col", None),
        P("row", "col"),
        P("row", "col", None, None, None),
        P("col", None, None, None),
        P("row", "col", None, None),
        P("row", "col", None, None, None),
    )
    out_specs = (
        P("row", "col", None, None, None),
        P("row", "col", None, None, None),
        P("row", "col", None, None),
    )
    return jax.shard_map(local, mesh=mesh, in_specs=in_specs, out_specs=out_specs, check_vma=False)
```

```python
import jax
import jax.numpy as jnp
from jax import lax
from jax.sharding import PartitionSpec as P
from jax.experimental import pallas as pl
from jax.experimental.pallas import tpu as pltpu


def from_behind(value, axis, steps):
    count = lax.axis_size(axis)
    initial, last = (max(0, -steps), min(count, count - steps))
    return lax.ppermute(value, axis, [(source, source + steps) for source in range(initial, last)])


def slot_tables(sources, targets, counts, sector_count):
    active_slot_list = lax.broadcasted_iota(jnp.int32, sources.shape, 2) < counts[:, :, None]
    sector_ids = lax.broadcasted_iota(jnp.int32, sources.shape + (sector_count,), 3)
    src_pick = sources[..., None] == sector_ids
    dst_pick = targets[..., None] == sector_ids
    return (src_pick, dst_pick, active_slot_list)


def forward_blocks(blocks, above_env, src_pick, dst_pick, active_slot_list):
    placed = (dst_pick & active_slot_list[..., None]).astype(jnp.float32)
    src_bf = src_pick.astype(jnp.bfloat16)
    gathered = jnp.einsum(
        "rckn,rcnbj->rckbj", src_bf, above_env, preferred_element_type=jnp.float32
    ).astype(jnp.bfloat16)
    products = jnp.einsum(
        "rckab,rckbj->rckaj", blocks, gathered, preferred_element_type=jnp.float32
    )
    return jnp.einsum("rckn,rckaj->rcnaj", placed, products, precision=lax.Precision.HIGHEST)


def backward_kernel(blocks, above_env, rounded, sources, targets, counts):
    site_count, slot_count = blocks.shape[:2]
    sector_count = above_env.shape[1]

    def body(src_ref, dst_ref, cnt_ref, blocks_ref, above_ref, rounded_ref, grads_ref, ret_ref, acc_ref):
        for site in range(site_count):
            acc_ref[...] = jnp.zeros(acc_ref.shape, jnp.float32)
            for slot in range(slot_count):
                place = site * slot_count + slot
                source = jnp.clip(src_ref[place], 0, sector_count - 1)
                target = jnp.clip(dst_ref[place], 0, sector_count - 1)
                live = slot < cnt_ref[site]
                picked = rounded_ref[site, target]
                gathered = above_ref[site, source]
                grad = lax.dot_general(
                    picked, gathered, (((1,), (1,)), ((), ())), preferred_element_type=jnp.float32
                )
                grads_ref[site, slot] = jnp.where(live, grad, 0.0).astype(grads_ref.dtype)
                contrib = lax.dot_general(
                    blocks_ref[site, slot], picked, (((0,), (0,)), ((), ())),
                    preferred_element_type=jnp.float32,
                )

                @pl.when(live)
                def _():
                    acc_ref[source] += contrib

            ret_ref[site] = acc_ref[...].astype(ret_ref.dtype)

    smem = pl.BlockSpec(memory_space=pltpu.SMEM)
    vmem = pl.BlockSpec(memory_space=pltpu.VMEM)
    return pl.pallas_call(
        body,
        in_specs=[smem, smem, smem, vmem, vmem, vmem],
        out_specs=(vmem, vmem),
        out_shape=(
            jax.ShapeDtypeStruct(blocks.shape, jnp.bfloat16),
            jax.ShapeDtypeStruct(above_env.shape, jnp.bfloat16),
        ),
        scratch_shapes=[pltpu.VMEM(above_env.shape[1:], jnp.float32)],
    )(sources, targets, counts, blocks, above_env, rounded)


def carry_kernel(fwd_b, bwd_b, factor):
    count, part, channel_count = fwd_b.shape

    def body(fwd_b_ref, bwd_b_ref, factor_ref, out_ref):
        state = jnp.zeros((part, channel_count), jnp.float32)
        for source in range(count):
            out_ref[source, 0] = state
            state = factor_ref[source] * state + fwd_b_ref[source]
        state = jnp.zeros((part, channel_count), jnp.float32)
        for source in reversed(range(count)):
            out_ref[source, 1] = state
            state = factor_ref[source] * state + bwd_b_ref[source]

    return pl.pallas_call(
        body,
        out_shape=jax.ShapeDtypeStruct((count, 2, part, channel_count), jnp.float32),
    )(fwd_b, bwd_b, factor)


def summary_kernel(fresh, cotangent, decay_col, factor_row, count):
    col_count, rows, channel_count = fresh.shape
    part = rows // count

    def body(fresh_ref, weight_ref, decay_ref, factor_ref, out_ref):
        for chunk in range(count):
            span = pl.ds(chunk * part, part)
            state = fresh_ref[0, span, :]
            for column in range(1, col_count):
                state = decay_ref[column, span, :] * state + fresh_ref[column, span, :]
            grad = weight_ref[col_count - 1, span, :]
            for column in reversed(range(col_count - 1)):
                grad = weight_ref[column, span, :] + decay_ref[column + 1, span, :] * grad
            grad = decay_ref[0, span, :] * grad
            out_ref[chunk, pl.ds(0, part), :] = state
            out_ref[chunk, pl.ds(part, part), :] = grad
            out_ref[chunk, pl.ds(2 * part, 1), :] = factor_ref[pl.ds(chunk, 1), :]

    return pl.pallas_call(
        body,
        out_shape=jax.ShapeDtypeStruct((count, 2 * part + 1, channel_count), jnp.float32),
    )(fresh, cotangent, decay_col, factor_row)


def fixup_kernel(fresh, cotangent, decay_col, carries):
    col_count, rows, channel_count = fresh.shape
    count, _, part, _ = carries.shape

    def body(fresh_ref, weight_ref, decay_ref, carry_ref, grad_ref, gate_ref):
        for chunk in range(count):
            span = pl.ds(chunk * part, part)
            grad = carry_ref[chunk, 1]
            grads = [None] * col_count
            for column in reversed(range(col_count)):
                grad = weight_ref[column, span, :] + grad
                grads[column] = grad
                grad_ref[column, span, :] = grad
                grad = decay_ref[column, span, :] * grad
            state = carry_ref[chunk, 0]
            for column in range(col_count):
                gate_ref[column, span, :] = jnp.sum(grads[column] * state, axis=-1, keepdims=True)
                state = decay_ref[column, span, :] * state + fresh_ref[column, span, :]

    return pl.pallas_call(
        body,
        out_shape=(
            jax.ShapeDtypeStruct((col_count, rows, channel_count), jnp.float32),
            jax.ShapeDtypeStruct((col_count, rows, 1), jnp.float32),
        ),
    )(fresh, cotangent, decay_col, carries)


def chain_scan(fresh, decay_rows, cotangent):
    row_count, col_count, flat_rows, channel_count = fresh.shape
    count = lax.axis_size("col")
    rows = row_count * flat_rows
    part = rows // count
    assert part * count == rows and part <= channel_count

    def by_column(value):
        return jnp.swapaxes(value, 0, 1).reshape(col_count, rows, -1)

    fresh_c = by_column(fresh)
    weight_c = by_column(cotangent)
    decay_c = by_column(decay_rows[..., None])
    factor = jnp.prod(jnp.swapaxes(decay_rows, 0, 1).reshape(col_count, count, part), 0)
    factor_row = jnp.pad(factor, ((0, 0), (0, channel_count - part)))
    payload = summary_kernel(fresh_c, weight_c, decay_c, factor_row, count)
    got = lax.all_to_all(payload, "col", 0, 0, tiled=True)
    carries = carry_kernel(got[:, :part], got[:, part : 2 * part], got[:, 2 * part, :part][..., None])
    ret = lax.all_to_all(carries, "col", 0, 0, tiled=True)
    grads, gates = fixup_kernel(fresh_c, weight_c, decay_c, ret)
    grads = jnp.swapaxes(grads.reshape(col_count, row_count, flat_rows, channel_count), 0, 1)
    gates = jnp.swapaxes(gates.reshape(col_count, row_count, flat_rows), 0, 1)
    return (grads, gates)


def local(blocks, sources, targets, counts, environment, top_boundary, decays, weights):
    row_count, col_count, sector_count, block_rows, channel_count = environment.shape
    flat_rows = sector_count * block_rows
    bottom = environment[row_count - 1]
    upper_env = from_behind(bottom, "row", 1)
    upper_env = jnp.where(lax.axis_index("row") == 0, top_boundary, upper_env)
    above_env = jnp.concatenate([upper_env[None], environment[: row_count - 1]], 0)
    src_pick, dst_pick, active_slot_list = slot_tables(sources, targets, counts, sector_count)
    transferred = forward_blocks(blocks, above_env, src_pick, dst_pick, active_slot_list)
    fresh = (environment.astype(jnp.float32) + transferred).reshape(
        row_count, col_count, flat_rows, channel_count
    )
    decay_rows = decays.reshape(row_count, col_count, flat_rows)
    cotangent = weights.reshape(row_count, col_count, flat_rows, channel_count)
    condition_derivative, gate_grad = chain_scan(fresh, decay_rows, cotangent)
    condition_derivative = condition_derivative.reshape(environment.shape)
    rounded = condition_derivative.astype(jnp.bfloat16)
    site_count = row_count * col_count
    grad_blocks, returned = backward_kernel(
        blocks.reshape((site_count,) + blocks.shape[2:]),
        above_env.reshape((site_count,) + above_env.shape[2:]),
        rounded.reshape((site_count,) + rounded.shape[2:]),
        sources.reshape(-1),
        targets.reshape(-1),
        counts.reshape(-1),
    )
    grad_blocks = grad_blocks.reshape(blocks.shape)
    returned = returned.reshape(environment.shape)
    below_rows = from_behind(returned[0], "row", -1)
    following_horizontals = jnp.concatenate([returned[1:], below_rows[None]], 0)
    grad_env = (condition_derivative + following_horizontals.astype(jnp.float32)).astype(
        jnp.bfloat16
    )
    grad_decays = gate_grad.reshape(decays.shape)
    return (grad_blocks, grad_env, grad_decays)


def solution(mesh):
    in_specs = (
        P("row", "col", None, None, None),
        P("row", "col", None),
        P("row", "col", None),
        P("row", "col"),
        P("row", "col", None, None, None),
        P("col", None, None, None),
        P("row", "col", None, None),
        P("row", "col", None, None, None),
    )
    out_specs = (
        P("row", "col", None, None, None),
        P("row", "col", None, None, None),
        P("row", "col", None, None),
    )
    return jax.shard_map(local, mesh=mesh, in_specs=in_specs, out_specs=out_specs, check_vma=False)
```

```python
import jax
import jax.numpy as jnp
from jax import lax
from jax.sharding import PartitionSpec as P
from jax.experimental import pallas as pl
from jax.experimental.pallas import tpu as pltpu


def from_behind(value, axis, steps):
    count = lax.axis_size(axis)
    initial, last = (max(0, -steps), min(count, count - steps))
    return lax.ppermute(value, axis, [(source, source + steps) for source in range(initial, last)])


def slot_tables(sources, targets, counts, sector_count):
    active_slot_list = lax.broadcasted_iota(jnp.int32, sources.shape, 2) < counts[:, :, None]
    sector_ids = lax.broadcasted_iota(jnp.int32, sources.shape + (sector_count,), 3)
    src_pick = sources[..., None] == sector_ids
    dst_pick = targets[..., None] == sector_ids
    return (src_pick, dst_pick, active_slot_list)


def forward_blocks(blocks, above_env, src_pick, dst_pick, active_slot_list):
    placed = (dst_pick & active_slot_list[..., None]).astype(jnp.float32)
    src_bf = src_pick.astype(jnp.bfloat16)
    gathered = jnp.einsum(
        "rckn,rcnbj->rckbj", src_bf, above_env, preferred_element_type=jnp.float32
    ).astype(jnp.bfloat16)
    products = jnp.einsum(
        "rckab,rckbj->rckaj", blocks, gathered, preferred_element_type=jnp.float32
    )
    return jnp.einsum("rckn,rckaj->rcnaj", placed, products, precision=lax.Precision.HIGHEST)


def backward_kernel(blocks, above_env, rounded, sources, targets, counts):
    site_count, slot_count = blocks.shape[:2]
    sector_count = above_env.shape[1]

    def body(src_ref, dst_ref, cnt_ref, blocks_ref, above_ref, rounded_ref, grads_ref, ret_ref, acc_ref):
        for site in range(site_count):
            acc_ref[...] = jnp.zeros(acc_ref.shape, jnp.float32)
            for slot in range(slot_count):
                place = site * slot_count + slot
                source = jnp.clip(src_ref[place], 0, sector_count - 1)
                target = jnp.clip(dst_ref[place], 0, sector_count - 1)
                live = slot < cnt_ref[site]
                picked = rounded_ref[site, target].astype(jnp.bfloat16)
                gathered = above_ref[site, source]
                grad = lax.dot_general(
                    picked, gathered, (((1,), (1,)), ((), ())), preferred_element_type=jnp.float32
                )
                grads_ref[site, slot] = jnp.where(live, grad, 0.0).astype(grads_ref.dtype)
                contrib = lax.dot_general(
                    blocks_ref[site, slot], picked, (((0,), (0,)), ((), ())),
                    preferred_element_type=jnp.float32,
                )

                @pl.when(live)
                def _():
                    acc_ref[source] += contrib

            ret_ref[site] = acc_ref[...].astype(ret_ref.dtype)

    smem = pl.BlockSpec(memory_space=pltpu.SMEM)
    vmem = pl.BlockSpec(memory_space=pltpu.VMEM)
    return pl.pallas_call(
        body,
        in_specs=[smem, smem, smem, vmem, vmem, vmem],
        out_specs=(vmem, vmem),
        out_shape=(
            jax.ShapeDtypeStruct(blocks.shape, jnp.bfloat16),
            jax.ShapeDtypeStruct(above_env.shape, jnp.bfloat16),
        ),
        scratch_shapes=[pltpu.VMEM(above_env.shape[1:], jnp.float32)],
    )(sources, targets, counts, blocks, above_env, rounded)


def carry_kernel(fwd_b, bwd_b, factor):
    count, part, channel_count = fwd_b.shape

    def body(fwd_b_ref, bwd_b_ref, factor_ref, out_ref):
        state = jnp.zeros((part, channel_count), jnp.float32)
        for source in range(count):
            out_ref[source, 0] = state
            state = factor_ref[source] * state + fwd_b_ref[source]
        state = jnp.zeros((part, channel_count), jnp.float32)
        for source in reversed(range(count)):
            out_ref[source, 1] = state
            state = factor_ref[source] * state + bwd_b_ref[source]

    return pl.pallas_call(
        body,
        out_shape=jax.ShapeDtypeStruct((count, 2, part, channel_count), jnp.float32),
    )(fwd_b, bwd_b, factor)


def summary_kernel(fresh, cotangent, decay_col, factor_row, count):
    col_count, rows, channel_count = fresh.shape
    part = rows // count

    def body(fresh_ref, weight_ref, decay_ref, factor_ref, out_ref):
        for chunk in range(count):
            span = pl.ds(chunk * part, part)
            state = fresh_ref[0, span, :]
            for column in range(1, col_count):
                state = decay_ref[column, span, :] * state + fresh_ref[column, span, :]
            grad = weight_ref[col_count - 1, span, :]
            for column in reversed(range(col_count - 1)):
                grad = weight_ref[column, span, :] + decay_ref[column + 1, span, :] * grad
            grad = decay_ref[0, span, :] * grad
            out_ref[chunk, pl.ds(0, part), :] = state
            out_ref[chunk, pl.ds(part, part), :] = grad
            out_ref[chunk, pl.ds(2 * part, 1), :] = factor_ref[pl.ds(chunk, 1), :]

    return pl.pallas_call(
        body,
        out_shape=jax.ShapeDtypeStruct((count, 2 * part + 1, channel_count), jnp.float32),
    )(fresh, cotangent, decay_col, factor_row)


def fixup_kernel(fresh, cotangent, decay_full, carries):
    col_count, rows, channel_count = fresh.shape
    count, _, part, _ = carries.shape

    def body(fresh_ref, weight_ref, decay_ref, carry_ref, grad_ref, prod_ref):
        for chunk in range(count):
            span = pl.ds(chunk * part, part)
            grad = carry_ref[chunk, 1]
            grads = [None] * col_count
            for column in reversed(range(col_count)):
                grad = weight_ref[column, span, :] + grad
                grads[column] = grad
                grad_ref[column, span, :] = grad
                grad = decay_ref[column, span, :] * grad
            state = carry_ref[chunk, 0]
            for column in range(col_count):
                prod_ref[column, span, :] = grads[column] * state
                state = decay_ref[column, span, :] * state + fresh_ref[column, span, :]

    grads, prods = pl.pallas_call(
        body,
        out_shape=(jax.ShapeDtypeStruct((col_count, rows, channel_count), jnp.float32),) * 2,
    )(fresh, cotangent, decay_full, carries)
    return (grads, jnp.sum(prods, -1))


def chain_scan(fresh, decay_rows, cotangent):
    row_count, col_count, flat_rows, channel_count = fresh.shape
    count = lax.axis_size("col")
    rows = row_count * flat_rows
    part = rows // count
    assert part * count == rows and part <= channel_count

    def by_column(value):
        return jnp.swapaxes(value, 0, 1).reshape(col_count, rows, -1)

    fresh_c = by_column(fresh)
    weight_c = by_column(cotangent)
    decay_c = jnp.broadcast_to(by_column(decay_rows[..., None]), fresh_c.shape)
    factor = jnp.prod(jnp.swapaxes(decay_rows, 0, 1).reshape(col_count, count, part), 0)
    factor_row = jnp.pad(factor, ((0, 0), (0, channel_count - part)))
    payload = summary_kernel(fresh_c, weight_c, decay_c, factor_row, count)
    got = lax.all_to_all(payload, "col", 0, 0, tiled=True)
    carries = carry_kernel(got[:, :part], got[:, part : 2 * part], got[:, 2 * part, :part][..., None])
    ret = lax.all_to_all(carries, "col", 0, 0, tiled=True)
    grads, gates = fixup_kernel(fresh_c, weight_c, decay_c, ret)
    grads = jnp.swapaxes(grads.reshape(col_count, row_count, flat_rows, channel_count), 0, 1)
    gates = jnp.swapaxes(gates.reshape(col_count, row_count, flat_rows), 0, 1)
    return (grads, gates)


def local(blocks, sources, targets, counts, environment, top_boundary, decays, weights):
    row_count, col_count, sector_count, block_rows, channel_count = environment.shape
    flat_rows = sector_count * block_rows
    bottom = environment[row_count - 1]
    upper_env = from_behind(bottom, "row", 1)
    upper_env = jnp.where(lax.axis_index("row") == 0, top_boundary, upper_env)
    above_env = jnp.concatenate([upper_env[None], environment[: row_count - 1]], 0)
    src_pick, dst_pick, active_slot_list = slot_tables(sources, targets, counts, sector_count)
    transferred = forward_blocks(blocks, above_env, src_pick, dst_pick, active_slot_list)
    fresh = (environment.astype(jnp.float32) + transferred).reshape(
        row_count, col_count, flat_rows, channel_count
    )
    decay_rows = decays.reshape(row_count, col_count, flat_rows)
    cotangent = weights.reshape(row_count, col_count, flat_rows, channel_count)
    condition_derivative, gate_grad = chain_scan(fresh, decay_rows, cotangent)
    condition_derivative = condition_derivative.reshape(environment.shape)
    rounded = condition_derivative.astype(jnp.bfloat16)
    site_count = row_count * col_count
    grad_blocks, returned = backward_kernel(
        blocks.reshape((site_count,) + blocks.shape[2:]),
        above_env.reshape((site_count,) + above_env.shape[2:]),
        condition_derivative.reshape((site_count,) + rounded.shape[2:]),
        sources.reshape(-1),
        targets.reshape(-1),
        counts.reshape(-1),
    )
    grad_blocks = grad_blocks.reshape(blocks.shape)
    returned = returned.reshape(environment.shape)
    below_rows = from_behind(returned[0], "row", -1)
    following_horizontals = jnp.concatenate([returned[1:], below_rows[None]], 0)
    grad_env = (condition_derivative + following_horizontals.astype(jnp.float32)).astype(
        jnp.bfloat16
    )
    grad_decays = gate_grad.reshape(decays.shape)
    return (grad_blocks, grad_env, grad_decays)


def solution(mesh):
    in_specs = (
        P("row", "col", None, None, None),
        P("row", "col", None),
        P("row", "col", None),
        P("row", "col"),
        P("row", "col", None, None, None),
        P("col", None, None, None),
        P("row", "col", None, None),
        P("row", "col", None, None, None),
    )
    out_specs = (
        P("row", "col", None, None, None),
        P("row", "col", None, None, None),
        P("row", "col", None, None),
    )
    return jax.shard_map(local, mesh=mesh, in_specs=in_specs, out_specs=out_specs, check_vma=False)
```

```python
import jax
import jax.numpy as jnp
from jax import lax
from jax.sharding import PartitionSpec as P
from jax.experimental import pallas as pl
from jax.experimental.pallas import tpu as pltpu


def from_behind(value, axis, steps):
    count = lax.axis_size(axis)
    initial, last = (max(0, -steps), min(count, count - steps))
    return lax.ppermute(value, axis, [(source, source + steps) for source in range(initial, last)])


def slot_tables(sources, targets, counts, sector_count):
    active_slot_list = lax.broadcasted_iota(jnp.int32, sources.shape, 2) < counts[:, :, None]
    sector_ids = lax.broadcasted_iota(jnp.int32, sources.shape + (sector_count,), 3)
    src_pick = sources[..., None] == sector_ids
    dst_pick = targets[..., None] == sector_ids
    return (src_pick, dst_pick, active_slot_list)


def forward_blocks(blocks, above_env, src_pick, dst_pick, active_slot_list):
    placed = (dst_pick & active_slot_list[..., None]).astype(jnp.float32)
    src_bf = src_pick.astype(jnp.bfloat16)
    gathered = jnp.einsum(
        "rckn,rcnbj->rckbj", src_bf, above_env, preferred_element_type=jnp.float32
    ).astype(jnp.bfloat16)
    products = jnp.einsum(
        "rckab,rckbj->rckaj", blocks, gathered, preferred_element_type=jnp.float32
    )
    return jnp.einsum("rckn,rckaj->rcnaj", placed, products, precision=lax.Precision.HIGHEST)


def backward_kernel(blocks, above_env, rounded, sources, targets, counts):
    site_count, slot_count = blocks.shape[:2]
    sector_count = above_env.shape[1]

    def body(src_ref, dst_ref, cnt_ref, blocks_ref, above_ref, rounded_ref, grads_ref, ret_ref, acc_ref):
        for site in range(site_count):
            acc_ref[...] = jnp.zeros(acc_ref.shape, jnp.float32)
            for slot in range(slot_count):
                place = site * slot_count + slot
                source = jnp.clip(src_ref[place], 0, sector_count - 1)
                target = jnp.clip(dst_ref[place], 0, sector_count - 1)
                live = slot < cnt_ref[site]
                picked = rounded_ref[site, target].astype(jnp.bfloat16)
                gathered = above_ref[site, source]
                grad = lax.dot_general(
                    picked, gathered, (((1,), (1,)), ((), ())), preferred_element_type=jnp.float32
                )
                grads_ref[site, slot] = jnp.where(live, grad, 0.0).astype(grads_ref.dtype)
                contrib = lax.dot_general(
                    blocks_ref[site, slot], picked, (((0,), (0,)), ((), ())),
                    preferred_element_type=jnp.float32,
                )

                @pl.when(live)
                def _():
                    acc_ref[source] += contrib

            ret_ref[site] = acc_ref[...].astype(ret_ref.dtype)

    smem = pl.BlockSpec(memory_space=pltpu.SMEM)
    vmem = pl.BlockSpec(memory_space=pltpu.VMEM)
    return pl.pallas_call(
        body,
        in_specs=[smem, smem, smem, vmem, vmem, vmem],
        out_specs=(vmem, vmem),
        out_shape=(
            jax.ShapeDtypeStruct(blocks.shape, jnp.bfloat16),
            jax.ShapeDtypeStruct(above_env.shape, jnp.bfloat16),
        ),
        scratch_shapes=[pltpu.VMEM(above_env.shape[1:], jnp.float32)],
    )(sources, targets, counts, blocks, above_env, rounded)


def carry_kernel(got, part):
    count, _, channel_count = got.shape

    def body(got_ref, out_ref):
        diagonal = lax.broadcasted_iota(jnp.int32, (part, channel_count), 0) == lax.broadcasted_iota(
            jnp.int32, (part, channel_count), 1
        )
        factors = []
        for source in range(count):
            row = got_ref[source, pl.ds(2 * part, 1), :]
            factors.append(jnp.sum(jnp.where(diagonal, row, 0.0), axis=-1, keepdims=True))
        state = jnp.zeros((part, channel_count), jnp.float32)
        for source in range(count):
            out_ref[source, pl.ds(0, part), :] = state
            state = factors[source] * state + got_ref[source, pl.ds(0, part), :]
        state = jnp.zeros((part, channel_count), jnp.float32)
        for source in reversed(range(count)):
            out_ref[source, pl.ds(part, part), :] = state
            state = factors[source] * state + got_ref[source, pl.ds(part, part), :]

    return pl.pallas_call(
        body,
        out_shape=jax.ShapeDtypeStruct((count, 2 * part, channel_count), jnp.float32),
    )(got)


def summary_kernel(fresh, cotangent, decay_col, factor_row, count):
    col_count, rows, channel_count = fresh.shape
    part = rows // count

    def body(fresh_ref, weight_ref, decay_ref, factor_ref, out_ref):
        for chunk in range(count):
            span = pl.ds(chunk * part, part)
            state = fresh_ref[0, span, :]
            for column in range(1, col_count):
                state = decay_ref[column, span, :] * state + fresh_ref[column, span, :]
            grad = weight_ref[col_count - 1, span, :]
            for column in reversed(range(col_count - 1)):
                grad = weight_ref[column, span, :] + decay_ref[column + 1, span, :] * grad
            grad = decay_ref[0, span, :] * grad
            out_ref[chunk, pl.ds(0, part), :] = state
            out_ref[chunk, pl.ds(part, part), :] = grad
            out_ref[chunk, pl.ds(2 * part, 1), :] = factor_ref[pl.ds(chunk, 1), :]

    return pl.pallas_call(
        body,
        out_shape=jax.ShapeDtypeStruct((count, 2 * part + 1, channel_count), jnp.float32),
    )(fresh, cotangent, decay_col, factor_row)


def fixup_kernel(fresh, cotangent, decay_full, carries):
    col_count, rows, channel_count = fresh.shape
    count = carries.shape[0]
    part = rows // count

    def body(fresh_ref, weight_ref, decay_ref, carry_ref, grad_ref, prod_ref):
        for chunk in range(count):
            span = pl.ds(chunk * part, part)
            grad = carry_ref[chunk, pl.ds(part, part), :]
            grads = [None] * col_count
            for column in reversed(range(col_count)):
                grad = weight_ref[column, span, :] + grad
                grads[column] = grad
                grad_ref[column, span, :] = grad
                grad = decay_ref[column, span, :] * grad
            state = carry_ref[chunk, pl.ds(0, part), :]
            for column in range(col_count):
                prod_ref[column, span, :] = grads[column] * state
                state = decay_ref[column, span, :] * state + fresh_ref[column, span, :]

    grads, prods = pl.pallas_call(
        body,
        out_shape=(jax.ShapeDtypeStruct((col_count, rows, channel_count), jnp.float32),) * 2,
    )(fresh, cotangent, decay_full, carries)
    return (grads, jnp.sum(prods, -1))


def chain_scan(fresh, decay_rows, cotangent):
    row_count, col_count, flat_rows, channel_count = fresh.shape
    count = lax.axis_size("col")
    rows = row_count * flat_rows
    part = rows // count
    assert part * count == rows and part <= channel_count

    def by_column(value):
        return jnp.swapaxes(value, 0, 1).reshape(col_count, rows, -1)

    fresh_c = by_column(fresh)
    weight_c = by_column(cotangent)
    decay_c = jnp.broadcast_to(by_column(decay_rows[..., None]), fresh_c.shape)
    factor = jnp.prod(jnp.swapaxes(decay_rows, 0, 1).reshape(col_count, count, part), 0)
    factor_row = jnp.pad(factor, ((0, 0), (0, channel_count - part)))
    payload = summary_kernel(fresh_c, weight_c, decay_c, factor_row, count)
    got = lax.all_to_all(payload, "col", 0, 0, tiled=True)
    carries = carry_kernel(got, part)
    ret = lax.all_to_all(carries, "col", 0, 0, tiled=True)
    grads, gates = fixup_kernel(fresh_c, weight_c, decay_c, ret)
    grads = jnp.swapaxes(grads.reshape(col_count, row_count, flat_rows, channel_count), 0, 1)
    gates = jnp.swapaxes(gates.reshape(col_count, row_count, flat_rows), 0, 1)
    return (grads, gates)


def local(blocks, sources, targets, counts, environment, top_boundary, decays, weights):
    row_count, col_count, sector_count, block_rows, channel_count = environment.shape
    flat_rows = sector_count * block_rows
    bottom = environment[row_count - 1]
    upper_env = from_behind(bottom, "row", 1)
    upper_env = jnp.where(lax.axis_index("row") == 0, top_boundary, upper_env)
    above_env = jnp.concatenate([upper_env[None], environment[: row_count - 1]], 0)
    src_pick, dst_pick, active_slot_list = slot_tables(sources, targets, counts, sector_count)
    transferred = forward_blocks(blocks, above_env, src_pick, dst_pick, active_slot_list)
    fresh = (environment.astype(jnp.float32) + transferred).reshape(
        row_count, col_count, flat_rows, channel_count
    )
    decay_rows = decays.reshape(row_count, col_count, flat_rows)
    cotangent = weights.reshape(row_count, col_count, flat_rows, channel_count)
    condition_derivative, gate_grad = chain_scan(fresh, decay_rows, cotangent)
    condition_derivative = condition_derivative.reshape(environment.shape)
    rounded = condition_derivative.astype(jnp.bfloat16)
    site_count = row_count * col_count
    grad_blocks, returned = backward_kernel(
        blocks.reshape((site_count,) + blocks.shape[2:]),
        above_env.reshape((site_count,) + above_env.shape[2:]),
        condition_derivative.reshape((site_count,) + rounded.shape[2:]),
        sources.reshape(-1),
        targets.reshape(-1),
        counts.reshape(-1),
    )
    grad_blocks = grad_blocks.reshape(blocks.shape)
    returned = returned.reshape(environment.shape)
    below_rows = from_behind(returned[0], "row", -1)
    following_horizontals = jnp.concatenate([returned[1:], below_rows[None]], 0)
    grad_env = (condition_derivative + following_horizontals.astype(jnp.float32)).astype(
        jnp.bfloat16
    )
    grad_decays = gate_grad.reshape(decays.shape)
    return (grad_blocks, grad_env, grad_decays)


def solution(mesh):
    in_specs = (
        P("row", "col", None, None, None),
        P("row", "col", None),
        P("row", "col", None),
        P("row", "col"),
        P("row", "col", None, None, None),
        P("col", None, None, None),
        P("row", "col", None, None),
        P("row", "col", None, None, None),
    )
    out_specs = (
        P("row", "col", None, None, None),
        P("row", "col", None, None, None),
        P("row", "col", None, None),
    )
    return jax.shard_map(local, mesh=mesh, in_specs=in_specs, out_specs=out_specs, check_vma=False)
```

```python
import jax
import jax.numpy as jnp
from jax import lax
from jax.sharding import PartitionSpec as P
from jax.experimental import pallas as pl
from jax.experimental.pallas import tpu as pltpu


def from_behind(value, axis, steps):
    count = lax.axis_size(axis)
    initial, last = (max(0, -steps), min(count, count - steps))
    return lax.ppermute(value, axis, [(source, source + steps) for source in range(initial, last)])


def forward_kernel(blocks, above_env, environment, sources, targets, counts):
    site_count, slot_count = blocks.shape[:2]
    sector_count = above_env.shape[1]

    def body(src_ref, dst_ref, cnt_ref, blocks_ref, above_ref, env_ref, fresh_ref):
        for site in range(site_count):
            fresh_ref[site] = env_ref[site].astype(jnp.float32)
            for slot in range(slot_count):
                place = site * slot_count + slot
                source = jnp.clip(src_ref[place], 0, sector_count - 1)
                target = jnp.clip(dst_ref[place], 0, sector_count - 1)
                product = jnp.dot(
                    blocks_ref[site, slot], above_ref[site, source], preferred_element_type=jnp.float32
                )

                @pl.when(slot < cnt_ref[site])
                def _():
                    fresh_ref[site, target] += product

    smem = pl.BlockSpec(memory_space=pltpu.SMEM)
    vmem = pl.BlockSpec(memory_space=pltpu.VMEM)
    return pl.pallas_call(
        body,
        in_specs=[smem, smem, smem, vmem, vmem, vmem],
        out_specs=vmem,
        out_shape=jax.ShapeDtypeStruct(environment.shape, jnp.float32),
    )(sources, targets, counts, blocks, above_env, environment)


def backward_kernel(blocks, above_env, rounded, sources, targets, counts):
    site_count, slot_count = blocks.shape[:2]
    sector_count = above_env.shape[1]

    def body(src_ref, dst_ref, cnt_ref, blocks_ref, above_ref, rounded_ref, grads_ref, ret_ref, acc_ref):
        for site in range(site_count):
            acc_ref[...] = jnp.zeros(acc_ref.shape, jnp.float32)
            for slot in range(slot_count):
                place = site * slot_count + slot
                source = jnp.clip(src_ref[place], 0, sector_count - 1)
                target = jnp.clip(dst_ref[place], 0, sector_count - 1)
                live = slot < cnt_ref[site]
                picked = rounded_ref[site, target].astype(jnp.bfloat16)
                gathered = above_ref[site, source]
                grad = lax.dot_general(
                    picked, gathered, (((1,), (1,)), ((), ())), preferred_element_type=jnp.float32
                )
                grads_ref[site, slot] = jnp.where(live, grad, 0.0).astype(grads_ref.dtype)
                contrib = lax.dot_general(
                    blocks_ref[site, slot], picked, (((0,), (0,)), ((), ())),
                    preferred_element_type=jnp.float32,
                )

                @pl.when(live)
                def _():
                    acc_ref[source] += contrib

            ret_ref[site] = acc_ref[...].astype(ret_ref.dtype)

    smem = pl.BlockSpec(memory_space=pltpu.SMEM)
    vmem = pl.BlockSpec(memory_space=pltpu.VMEM)
    return pl.pallas_call(
        body,
        in_specs=[smem, smem, smem, vmem, vmem, vmem],
        out_specs=(vmem, vmem),
        out_shape=(
            jax.ShapeDtypeStruct(blocks.shape, jnp.bfloat16),
            jax.ShapeDtypeStruct(above_env.shape, jnp.bfloat16),
        ),
        scratch_shapes=[pltpu.VMEM(above_env.shape[1:], jnp.float32)],
    )(sources, targets, counts, blocks, above_env, rounded)


def carry_kernel(got, part):
    count, _, channel_count = got.shape

    def body(got_ref, out_ref):
        diagonal = lax.broadcasted_iota(jnp.int32, (part, channel_count), 0) == lax.broadcasted_iota(
            jnp.int32, (part, channel_count), 1
        )
        factors = []
        for source in range(count):
            row = got_ref[source, pl.ds(2 * part, 1), :]
            factors.append(jnp.sum(jnp.where(diagonal, row, 0.0), axis=-1, keepdims=True))
        state = jnp.zeros((part, channel_count), jnp.float32)
        for source in range(count):
            out_ref[source, pl.ds(0, part), :] = state
            state = factors[source] * state + got_ref[source, pl.ds(0, part), :]
        state = jnp.zeros((part, channel_count), jnp.float32)
        for source in reversed(range(count)):
            out_ref[source, pl.ds(part, part), :] = state
            state = factors[source] * state + got_ref[source, pl.ds(part, part), :]

    return pl.pallas_call(
        body,
        out_shape=jax.ShapeDtypeStruct((count, 2 * part, channel_count), jnp.float32),
    )(got)


def summary_kernel(fresh, cotangent, decay_col, factor_row, count):
    col_count, rows, channel_count = fresh.shape
    part = rows // count

    def body(fresh_ref, weight_ref, decay_ref, factor_ref, out_ref):
        for chunk in range(count):
            span = pl.ds(chunk * part, part)
            state = fresh_ref[0, span, :]
            for column in range(1, col_count):
                state = decay_ref[column, span, :] * state + fresh_ref[column, span, :]
            grad = weight_ref[col_count - 1, span, :]
            for column in reversed(range(col_count - 1)):
                grad = weight_ref[column, span, :] + decay_ref[column + 1, span, :] * grad
            grad = decay_ref[0, span, :] * grad
            out_ref[chunk, pl.ds(0, part), :] = state
            out_ref[chunk, pl.ds(part, part), :] = grad
            out_ref[chunk, pl.ds(2 * part, 1), :] = factor_ref[pl.ds(chunk, 1), :]

    return pl.pallas_call(
        body,
        out_shape=jax.ShapeDtypeStruct((count, 2 * part + 1, channel_count), jnp.float32),
    )(fresh, cotangent, decay_col, factor_row)


def fixup_kernel(fresh, cotangent, decay_full, carries):
    col_count, rows, channel_count = fresh.shape
    count = carries.shape[0]
    part = rows // count

    def body(fresh_ref, weight_ref, decay_ref, carry_ref, grad_ref, prod_ref):
        for chunk in range(count):
            span = pl.ds(chunk * part, part)
            grad = carry_ref[chunk, pl.ds(part, part), :]
            grads = [None] * col_count
            for column in reversed(range(col_count)):
                grad = weight_ref[column, span, :] + grad
                grads[column] = grad
                grad_ref[column, span, :] = grad
                grad = decay_ref[column, span, :] * grad
            state = carry_ref[chunk, pl.ds(0, part), :]
            for column in range(col_count):
                prod_ref[column, span, :] = grads[column] * state
                state = decay_ref[column, span, :] * state + fresh_ref[column, span, :]

    grads, prods = pl.pallas_call(
        body,
        out_shape=(jax.ShapeDtypeStruct((col_count, rows, channel_count), jnp.float32),) * 2,
    )(fresh, cotangent, decay_full, carries)
    return (grads, jnp.sum(prods, -1))


def chain_scan(fresh, decay_rows, cotangent):
    row_count, col_count, flat_rows, channel_count = fresh.shape
    count = lax.axis_size("col")
    rows = row_count * flat_rows
    part = rows // count
    assert part * count == rows and part <= channel_count

    def by_column(value):
        return jnp.swapaxes(value, 0, 1).reshape(col_count, rows, -1)

    fresh_c = by_column(fresh)
    weight_c = by_column(cotangent)
    decay_c = jnp.broadcast_to(by_column(decay_rows[..., None]), fresh_c.shape)
    factor = jnp.prod(jnp.swapaxes(decay_rows, 0, 1).reshape(col_count, count, part), 0)
    factor_row = jnp.pad(factor, ((0, 0), (0, channel_count - part)))
    payload = summary_kernel(fresh_c, weight_c, decay_c, factor_row, count)
    got = lax.all_to_all(payload, "col", 0, 0, tiled=True)
    carries = carry_kernel(got, part)
    ret = lax.all_to_all(carries, "col", 0, 0, tiled=True)
    grads, gates = fixup_kernel(fresh_c, weight_c, decay_c, ret)
    grads = jnp.swapaxes(grads.reshape(col_count, row_count, flat_rows, channel_count), 0, 1)
    gates = jnp.swapaxes(gates.reshape(col_count, row_count, flat_rows), 0, 1)
    return (grads, gates)


def local(blocks, sources, targets, counts, environment, top_boundary, decays, weights):
    row_count, col_count, sector_count, block_rows, channel_count = environment.shape
    flat_rows = sector_count * block_rows
    bottom = environment[row_count - 1]
    upper_env = from_behind(bottom, "row", 1)
    upper_env = jnp.where(lax.axis_index("row") == 0, top_boundary, upper_env)
    above_env = jnp.concatenate([upper_env[None], environment[: row_count - 1]], 0)
    site_count = row_count * col_count

    def by_site(value):
        return value.reshape((site_count,) + value.shape[2:])

    fresh = forward_kernel(
        by_site(blocks),
        by_site(above_env),
        by_site(environment),
        sources.reshape(-1),
        targets.reshape(-1),
        counts.reshape(-1),
    ).reshape(row_count, col_count, flat_rows, channel_count)
    decay_rows = decays.reshape(row_count, col_count, flat_rows)
    cotangent = weights.reshape(row_count, col_count, flat_rows, channel_count)
    condition_derivative, gate_grad = chain_scan(fresh, decay_rows, cotangent)
    condition_derivative = condition_derivative.reshape(environment.shape)
    grad_blocks, returned = backward_kernel(
        blocks.reshape((site_count,) + blocks.shape[2:]),
        above_env.reshape((site_count,) + above_env.shape[2:]),
        condition_derivative.reshape((site_count,) + condition_derivative.shape[2:]),
        sources.reshape(-1),
        targets.reshape(-1),
        counts.reshape(-1),
    )
    grad_blocks = grad_blocks.reshape(blocks.shape)
    returned = returned.reshape(environment.shape)
    below_rows = from_behind(returned[0], "row", -1)
    following_horizontals = jnp.concatenate([returned[1:], below_rows[None]], 0)
    grad_env = (condition_derivative + following_horizontals.astype(jnp.float32)).astype(
        jnp.bfloat16
    )
    grad_decays = gate_grad.reshape(decays.shape)
    return (grad_blocks, grad_env, grad_decays)


def solution(mesh):
    in_specs = (
        P("row", "col", None, None, None),
        P("row", "col", None),
        P("row", "col", None),
        P("row", "col"),
        P("row", "col", None, None, None),
        P("col", None, None, None),
        P("row", "col", None, None),
        P("row", "col", None, None, None),
    )
    out_specs = (
        P("row", "col", None, None, None),
        P("row", "col", None, None, None),
        P("row", "col", None, None),
    )
    return jax.shard_map(local, mesh=mesh, in_specs=in_specs, out_specs=out_specs, check_vma=False)
```

```python
import jax
import jax.numpy as jnp
from jax import lax
from jax.sharding import PartitionSpec as P
from jax.experimental import pallas as pl
from jax.experimental.pallas import tpu as pltpu


def from_behind(value, axis, steps):
    count = lax.axis_size(axis)
    initial, last = (max(0, -steps), min(count, count - steps))
    return lax.ppermute(value, axis, [(source, source + steps) for source in range(initial, last)])


def forward_kernel(blocks, above_env, environment, sources, targets, counts):
    site_count, slot_count = blocks.shape[:2]
    sector_count = above_env.shape[1]

    def body(src_ref, dst_ref, cnt_ref, blocks_ref, above_ref, env_ref, fresh_ref):
        for site in range(site_count):
            fresh_ref[site] = env_ref[site].astype(jnp.float32)
            for slot in range(slot_count):
                place = site * slot_count + slot
                source = jnp.clip(src_ref[place], 0, sector_count - 1)
                target = jnp.clip(dst_ref[place], 0, sector_count - 1)
                product = jnp.dot(
                    blocks_ref[site, slot], above_ref[site, source], preferred_element_type=jnp.float32
                )
                fresh_ref[site, target] += jnp.where(slot < cnt_ref[site], product, 0.0)

    smem = pl.BlockSpec(memory_space=pltpu.SMEM)
    vmem = pl.BlockSpec(memory_space=pltpu.VMEM)
    return pl.pallas_call(
        body,
        in_specs=[smem, smem, smem, vmem, vmem, vmem],
        out_specs=vmem,
        out_shape=jax.ShapeDtypeStruct(environment.shape, jnp.float32),
    )(sources, targets, counts, blocks, above_env, environment)


def backward_kernel(blocks, above_env, rounded, sources, targets, counts):
    site_count, slot_count = blocks.shape[:2]
    sector_count = above_env.shape[1]

    def body(src_ref, dst_ref, cnt_ref, blocks_ref, above_ref, rounded_ref, grads_ref, ret_ref, acc_ref):
        for site in range(site_count):
            acc_ref[...] = jnp.zeros(acc_ref.shape, jnp.float32)
            for slot in range(slot_count):
                place = site * slot_count + slot
                source = jnp.clip(src_ref[place], 0, sector_count - 1)
                target = jnp.clip(dst_ref[place], 0, sector_count - 1)
                live = slot < cnt_ref[site]
                picked = rounded_ref[site, target].astype(jnp.bfloat16)
                gathered = above_ref[site, source]
                grad = lax.dot_general(
                    picked, gathered, (((1,), (1,)), ((), ())), preferred_element_type=jnp.float32
                )
                grads_ref[site, slot] = jnp.where(live, grad, 0.0).astype(grads_ref.dtype)
                contrib = lax.dot_general(
                    blocks_ref[site, slot], picked, (((0,), (0,)), ((), ())),
                    preferred_element_type=jnp.float32,
                )
                acc_ref[source] += jnp.where(live, contrib, 0.0)

            ret_ref[site] = acc_ref[...].astype(ret_ref.dtype)

    smem = pl.BlockSpec(memory_space=pltpu.SMEM)
    vmem = pl.BlockSpec(memory_space=pltpu.VMEM)
    return pl.pallas_call(
        body,
        in_specs=[smem, smem, smem, vmem, vmem, vmem],
        out_specs=(vmem, vmem),
        out_shape=(
            jax.ShapeDtypeStruct(blocks.shape, jnp.bfloat16),
            jax.ShapeDtypeStruct(above_env.shape, jnp.bfloat16),
        ),
        scratch_shapes=[pltpu.VMEM(above_env.shape[1:], jnp.float32)],
    )(sources, targets, counts, blocks, above_env, rounded)


def carry_kernel(got, part):
    count, _, channel_count = got.shape

    def body(got_ref, out_ref):
        diagonal = lax.broadcasted_iota(jnp.int32, (part, channel_count), 0) == lax.broadcasted_iota(
            jnp.int32, (part, channel_count), 1
        )
        factors = []
        for source in range(count):
            row = got_ref[source, pl.ds(2 * part, 1), :]
            factors.append(jnp.sum(jnp.where(diagonal, row, 0.0), axis=-1, keepdims=True))
        state = jnp.zeros((part, channel_count), jnp.float32)
        for source in range(count):
            out_ref[source, pl.ds(0, part), :] = state
            state = factors[source] * state + got_ref[source, pl.ds(0, part), :]
        state = jnp.zeros((part, channel_count), jnp.float32)
        for source in reversed(range(count)):
            out_ref[source, pl.ds(part, part), :] = state
            state = factors[source] * state + got_ref[source, pl.ds(part, part), :]

    return pl.pallas_call(
        body,
        out_shape=jax.ShapeDtypeStruct((count, 2 * part, channel_count), jnp.float32),
    )(got)


def summary_kernel(fresh, cotangent, decay_col, factor_row, count):
    col_count, rows, channel_count = fresh.shape
    part = rows // count

    def body(fresh_ref, weight_ref, decay_ref, factor_ref, out_ref):
        for chunk in range(count):
            span = pl.ds(chunk * part, part)
            state = fresh_ref[0, span, :]
            for column in range(1, col_count):
                state = decay_ref[column, span, :] * state + fresh_ref[column, span, :]
            grad = weight_ref[col_count - 1, span, :]
            for column in reversed(range(col_count - 1)):
                grad = weight_ref[column, span, :] + decay_ref[column + 1, span, :] * grad
            grad = decay_ref[0, span, :] * grad
            out_ref[chunk, pl.ds(0, part), :] = state
            out_ref[chunk, pl.ds(part, part), :] = grad
            out_ref[chunk, pl.ds(2 * part, 1), :] = factor_ref[pl.ds(chunk, 1), :]

    return pl.pallas_call(
        body,
        out_shape=jax.ShapeDtypeStruct((count, 2 * part + 1, channel_count), jnp.float32),
    )(fresh, cotangent, decay_col, factor_row)


def fixup_kernel(fresh, cotangent, decay_full, carries):
    col_count, rows, channel_count = fresh.shape
    count = carries.shape[0]
    part = rows // count

    def body(fresh_ref, weight_ref, decay_ref, carry_ref, grad_ref, prod_ref):
        for chunk in range(count):
            span = pl.ds(chunk * part, part)
            grad = carry_ref[chunk, pl.ds(part, part), :]
            grads = [None] * col_count
            for column in reversed(range(col_count)):
                grad = weight_ref[column, span, :] + grad
                grads[column] = grad
                grad_ref[column, span, :] = grad
                grad = decay_ref[column, span, :] * grad
            state = carry_ref[chunk, pl.ds(0, part), :]
            for column in range(col_count):
                prod_ref[column, span, :] = grads[column] * state
                state = decay_ref[column, span, :] * state + fresh_ref[column, span, :]

    grads, prods = pl.pallas_call(
        body,
        out_shape=(jax.ShapeDtypeStruct((col_count, rows, channel_count), jnp.float32),) * 2,
    )(fresh, cotangent, decay_full, carries)
    return (grads, jnp.sum(prods, -1))


def chain_scan(fresh, decay_rows, cotangent):
    row_count, col_count, flat_rows, channel_count = fresh.shape
    count = lax.axis_size("col")
    rows = row_count * flat_rows
    part = rows // count
    assert part * count == rows and part <= channel_count

    def by_column(value):
        return jnp.swapaxes(value, 0, 1).reshape(col_count, rows, -1)

    fresh_c = by_column(fresh)
    weight_c = by_column(cotangent)
    decay_c = jnp.broadcast_to(by_column(decay_rows[..., None]), fresh_c.shape)
    factor = jnp.prod(jnp.swapaxes(decay_rows, 0, 1).reshape(col_count, count, part), 0)
    factor_row = jnp.pad(factor, ((0, 0), (0, channel_count - part)))
    payload = summary_kernel(fresh_c, weight_c, decay_c, factor_row, count)
    got = lax.all_to_all(payload, "col", 0, 0, tiled=True)
    carries = carry_kernel(got, part)
    ret = lax.all_to_all(carries, "col", 0, 0, tiled=True)
    grads, gates = fixup_kernel(fresh_c, weight_c, decay_c, ret)
    grads = jnp.swapaxes(grads.reshape(col_count, row_count, flat_rows, channel_count), 0, 1)
    gates = jnp.swapaxes(gates.reshape(col_count, row_count, flat_rows), 0, 1)
    return (grads, gates)


def local(blocks, sources, targets, counts, environment, top_boundary, decays, weights):
    row_count, col_count, sector_count, block_rows, channel_count = environment.shape
    flat_rows = sector_count * block_rows
    bottom = environment[row_count - 1]
    upper_env = from_behind(bottom, "row", 1)
    upper_env = jnp.where(lax.axis_index("row") == 0, top_boundary, upper_env)
    above_env = jnp.concatenate([upper_env[None], environment[: row_count - 1]], 0)
    site_count = row_count * col_count

    def by_site(value):
        return value.reshape((site_count,) + value.shape[2:])

    fresh = forward_kernel(
        by_site(blocks),
        by_site(above_env),
        by_site(environment),
        sources.reshape(-1),
        targets.reshape(-1),
        counts.reshape(-1),
    ).reshape(row_count, col_count, flat_rows, channel_count)
    decay_rows = decays.reshape(row_count, col_count, flat_rows)
    cotangent = weights.reshape(row_count, col_count, flat_rows, channel_count)
    condition_derivative, gate_grad = chain_scan(fresh, decay_rows, cotangent)
    condition_derivative = condition_derivative.reshape(environment.shape)
    grad_blocks, returned = backward_kernel(
        blocks.reshape((site_count,) + blocks.shape[2:]),
        above_env.reshape((site_count,) + above_env.shape[2:]),
        condition_derivative.reshape((site_count,) + condition_derivative.shape[2:]),
        sources.reshape(-1),
        targets.reshape(-1),
        counts.reshape(-1),
    )
    grad_blocks = grad_blocks.reshape(blocks.shape)
    returned = returned.reshape(environment.shape)
    below_rows = from_behind(returned[0], "row", -1)
    following_horizontals = jnp.concatenate([returned[1:], below_rows[None]], 0)
    grad_env = (condition_derivative + following_horizontals.astype(jnp.float32)).astype(
        jnp.bfloat16
    )
    grad_decays = gate_grad.reshape(decays.shape)
    return (grad_blocks, grad_env, grad_decays)


def solution(mesh):
    in_specs = (
        P("row", "col", None, None, None),
        P("row", "col", None),
        P("row", "col", None),
        P("row", "col"),
        P("row", "col", None, None, None),
        P("col", None, None, None),
        P("row", "col", None, None),
        P("row", "col", None, None, None),
    )
    out_specs = (
        P("row", "col", None, None, None),
        P("row", "col", None, None, None),
        P("row", "col", None, None),
    )
    return jax.shard_map(local, mesh=mesh, in_specs=in_specs, out_specs=out_specs, check_vma=False)
```

```python
import jax
import jax.numpy as jnp
from jax import lax
from jax.sharding import PartitionSpec as P
from jax.experimental import pallas as pl
from jax.experimental.pallas import tpu as pltpu


def from_behind(value, axis, steps):
    count = lax.axis_size(axis)
    initial, last = (max(0, -steps), min(count, count - steps))
    return lax.ppermute(value, axis, [(source, source + steps) for source in range(initial, last)])


def forward_kernel(blocks, top_env, received_env, environment, decays, first, sources, targets, counts):
    site_count, slot_count = blocks.shape[:2]
    sector_count = environment.shape[1]

    def body(
        src_ref, dst_ref, cnt_ref, first_ref, blocks_ref, top_ref, recv_ref, env_ref, decay_ref,
        fresh_ref, decay_out_ref,
    ):
        for site in range(site_count):
            for sector in range(sector_count):
                row = decay_ref[site, pl.ds(sector, 1), :]
                decay_out_ref[site, sector] = jnp.transpose(jnp.broadcast_to(row, decay_out_ref.shape[2:]))
            fresh_ref[site] = env_ref[site].astype(jnp.float32)
            for slot in range(slot_count):
                place = site * slot_count + slot
                source = jnp.clip(src_ref[place], 0, sector_count - 1)
                target = jnp.clip(dst_ref[place], 0, sector_count - 1)
                above = jnp.where(first_ref[0] > 0, top_ref[site, source], recv_ref[site, source])
                product = jnp.dot(blocks_ref[site, slot], above, preferred_element_type=jnp.float32)
                fresh_ref[site, target] += jnp.where(slot < cnt_ref[site], product, 0.0)

    smem = pl.BlockSpec(memory_space=pltpu.SMEM)
    vmem = pl.BlockSpec(memory_space=pltpu.VMEM)
    return pl.pallas_call(
        body,
        in_specs=[smem] * 4 + [vmem] * 5,
        out_specs=(vmem, vmem),
        out_shape=(
            jax.ShapeDtypeStruct(environment.shape, jnp.float32),
            jax.ShapeDtypeStruct(environment.shape, jnp.float32),
        ),
    )(sources, targets, counts, first, blocks, top_env, received_env, environment, decays)


def backward_kernel(blocks, top_env, received_env, rounded, first, sources, targets, counts):
    site_count, slot_count = blocks.shape[:2]
    sector_count = top_env.shape[1]

    def body(src_ref, dst_ref, cnt_ref, first_ref, blocks_ref, top_ref, recv_ref, rounded_ref, grads_ref, ret_ref, acc_ref):
        for site in range(site_count):
            acc_ref[...] = jnp.zeros(acc_ref.shape, jnp.float32)
            for slot in range(slot_count):
                place = site * slot_count + slot
                source = jnp.clip(src_ref[place], 0, sector_count - 1)
                target = jnp.clip(dst_ref[place], 0, sector_count - 1)
                live = slot < cnt_ref[site]
                picked = rounded_ref[site, target].astype(jnp.bfloat16)
                gathered = jnp.where(first_ref[0] > 0, top_ref[site, source], recv_ref[site, source])
                grad = lax.dot_general(
                    picked, gathered, (((1,), (1,)), ((), ())), preferred_element_type=jnp.float32
                )
                grads_ref[site, slot] = jnp.where(live, grad, 0.0).astype(grads_ref.dtype)
                contrib = lax.dot_general(
                    blocks_ref[site, slot], picked, (((0,), (0,)), ((), ())),
                    preferred_element_type=jnp.float32,
                )
                acc_ref[source] += jnp.where(live, contrib, 0.0)

            ret_ref[site] = acc_ref[...].astype(ret_ref.dtype)

    smem = pl.BlockSpec(memory_space=pltpu.SMEM)
    vmem = pl.BlockSpec(memory_space=pltpu.VMEM)
    return pl.pallas_call(
        body,
        in_specs=[smem] * 4 + [vmem] * 4,
        out_specs=(vmem, vmem),
        out_shape=(
            jax.ShapeDtypeStruct(blocks.shape, jnp.bfloat16),
            jax.ShapeDtypeStruct(top_env.shape, jnp.bfloat16),
        ),
        scratch_shapes=[pltpu.VMEM(top_env.shape[1:], jnp.float32)],
    )(sources, targets, counts, first, blocks, top_env, received_env, rounded)


def carry_kernel(got, part):
    count, _, channel_count = got.shape

    def body(got_ref, out_ref):
        diagonal = lax.broadcasted_iota(jnp.int32, (part, channel_count), 0) == lax.broadcasted_iota(
            jnp.int32, (part, channel_count), 1
        )
        factors = []
        for source in range(count):
            row = got_ref[source, pl.ds(2 * part, 1), :]
            factors.append(jnp.sum(jnp.where(diagonal, row, 0.0), axis=-1, keepdims=True))
        state = jnp.zeros((part, channel_count), jnp.float32)
        for source in range(count):
            out_ref[source, pl.ds(0, part), :] = state
            state = factors[source] * state + got_ref[source, pl.ds(0, part), :]
        state = jnp.zeros((part, channel_count), jnp.float32)
        for source in reversed(range(count)):
            out_ref[source, pl.ds(part, part), :] = state
            state = factors[source] * state + got_ref[source, pl.ds(part, part), :]

    return pl.pallas_call(
        body,
        out_shape=jax.ShapeDtypeStruct((count, 2 * part, channel_count), jnp.float32),
    )(got)


def summary_kernel(fresh, cotangent, decay_col, factor_row, count):
    col_count, rows, channel_count = fresh.shape
    part = rows // count

    def body(fresh_ref, weight_ref, decay_ref, factor_ref, out_ref):
        for chunk in range(count):
            span = pl.ds(chunk * part, part)
            state = fresh_ref[0, span, :]
            for column in range(1, col_count):
                state = decay_ref[column, span, :] * state + fresh_ref[column, span, :]
            grad = weight_ref[col_count - 1, span, :]
            for column in reversed(range(col_count - 1)):
                grad = weight_ref[column, span, :] + decay_ref[column + 1, span, :] * grad
            grad = decay_ref[0, span, :] * grad
            out_ref[chunk, pl.ds(0, part), :] = state
            out_ref[chunk, pl.ds(part, part), :] = grad
            out_ref[chunk, pl.ds(2 * part, 1), :] = factor_ref[pl.ds(chunk, 1), :]

    return pl.pallas_call(
        body,
        out_shape=jax.ShapeDtypeStruct((count, 2 * part + 1, channel_count), jnp.float32),
    )(fresh, cotangent, decay_col, factor_row)


def fixup_kernel(fresh, cotangent, decay_full, carries):
    col_count, rows, channel_count = fresh.shape
    count = carries.shape[0]
    part = rows // count

    def body(fresh_ref, weight_ref, decay_ref, carry_ref, grad_ref, prod_ref):
        for chunk in range(count):
            span = pl.ds(chunk * part, part)
            grad = carry_ref[chunk, pl.ds(part, part), :]
            grads = [None] * col_count
            for column in reversed(range(col_count)):
                grad = weight_ref[column, span, :] + grad
                grads[column] = grad
                grad_ref[column, span, :] = grad
                grad = decay_ref[column, span, :] * grad
            state = carry_ref[chunk, pl.ds(0, part), :]
            for column in range(col_count):
                prod_ref[column, span, :] = grads[column] * state
                state = decay_ref[column, span, :] * state + fresh_ref[column, span, :]

    grads, prods = pl.pallas_call(
        body,
        out_shape=(jax.ShapeDtypeStruct((col_count, rows, channel_count), jnp.float32),) * 2,
    )(fresh, cotangent, decay_full, carries)
    return (grads, jnp.sum(prods, -1))


def chain_scan(fresh, decay_rows, decay_full, cotangent):
    row_count, col_count, flat_rows, channel_count = fresh.shape
    count = lax.axis_size("col")
    rows = row_count * flat_rows
    part = rows // count
    assert part * count == rows and part <= channel_count

    def by_column(value):
        return jnp.swapaxes(value, 0, 1).reshape(col_count, rows, -1)

    fresh_c = by_column(fresh)
    weight_c = by_column(cotangent)
    decay_c = by_column(decay_full)
    factor = jnp.prod(jnp.swapaxes(decay_rows, 0, 1).reshape(col_count, count, part), 0)
    factor_row = jnp.pad(factor, ((0, 0), (0, channel_count - part)))
    payload = summary_kernel(fresh_c, weight_c, decay_c, factor_row, count)
    got = lax.all_to_all(payload, "col", 0, 0, tiled=True)
    carries = carry_kernel(got, part)
    ret = lax.all_to_all(carries, "col", 0, 0, tiled=True)
    grads, gates = fixup_kernel(fresh_c, weight_c, decay_c, ret)
    grads = jnp.swapaxes(grads.reshape(col_count, row_count, flat_rows, channel_count), 0, 1)
    gates = jnp.swapaxes(gates.reshape(col_count, row_count, flat_rows), 0, 1)
    return (grads, gates)


def local(blocks, sources, targets, counts, environment, top_boundary, decays, weights):
    row_count, col_count, sector_count, block_rows, channel_count = environment.shape
    flat_rows = sector_count * block_rows
    bottom = environment[row_count - 1]
    upper_env = from_behind(bottom, "row", 1)
    received_env = jnp.concatenate([upper_env[None], environment[: row_count - 1]], 0)
    top_env = jnp.concatenate([top_boundary[None], environment[: row_count - 1]], 0)
    first = (lax.axis_index("row") == 0).astype(jnp.int32).reshape(1)
    site_count = row_count * col_count

    def by_site(value):
        return value.reshape((site_count,) + value.shape[2:])

    fresh, decay_full = forward_kernel(
        by_site(blocks),
        by_site(top_env),
        by_site(received_env),
        by_site(environment),
        by_site(decays),
        first,
        sources.reshape(-1),
        targets.reshape(-1),
        counts.reshape(-1),
    )
    fresh = fresh.reshape(row_count, col_count, flat_rows, channel_count)
    decay_full = decay_full.reshape(row_count, col_count, flat_rows, channel_count)
    decay_rows = decays.reshape(row_count, col_count, flat_rows)
    cotangent = weights.reshape(row_count, col_count, flat_rows, channel_count)
    condition_derivative, gate_grad = chain_scan(fresh, decay_rows, decay_full, cotangent)
    condition_derivative = condition_derivative.reshape(environment.shape)
    grad_blocks, returned = backward_kernel(
        by_site(blocks),
        by_site(top_env),
        by_site(received_env),
        by_site(condition_derivative),
        first,
        sources.reshape(-1),
        targets.reshape(-1),
        counts.reshape(-1),
    )
    grad_blocks = grad_blocks.reshape(blocks.shape)
    returned = returned.reshape(environment.shape)
    below_rows = from_behind(returned[0], "row", -1)
    following_horizontals = jnp.concatenate([returned[1:], below_rows[None]], 0)
    grad_env = (condition_derivative + following_horizontals.astype(jnp.float32)).astype(
        jnp.bfloat16
    )
    grad_decays = gate_grad.reshape(decays.shape)
    return (grad_blocks, grad_env, grad_decays)


def solution(mesh):
    in_specs = (
        P("row", "col", None, None, None),
        P("row", "col", None),
        P("row", "col", None),
        P("row", "col"),
        P("row", "col", None, None, None),
        P("col", None, None, None),
        P("row", "col", None, None),
        P("row", "col", None, None, None),
    )
    out_specs = (
        P("row", "col", None, None, None),
        P("row", "col", None, None, None),
        P("row", "col", None, None),
    )
    return jax.shard_map(local, mesh=mesh, in_specs=in_specs, out_specs=out_specs, check_vma=False)
```

```python
import jax
import jax.numpy as jnp
from jax import lax
from jax.sharding import PartitionSpec as P
from jax.experimental import pallas as pl
from jax.experimental.pallas import tpu as pltpu


def from_behind(value, axis, steps):
    count = lax.axis_size(axis)
    initial, last = (max(0, -steps), min(count, count - steps))
    return lax.ppermute(value, axis, [(source, source + steps) for source in range(initial, last)])


def forward_kernel(blocks, top_env, received_env, environment, decays, first, sources, targets, counts):
    site_count, slot_count = blocks.shape[:2]
    sector_count = environment.shape[1]

    def body(
        src_ref, dst_ref, cnt_ref, first_ref, blocks_ref, top_ref, recv_ref, env_ref, decay_ref,
        fresh_ref, decay_out_ref,
    ):
        for site in range(site_count):
            for sector in range(sector_count):
                row = decay_ref[site, pl.ds(sector, 1), :]
                decay_out_ref[site, sector] = jnp.transpose(jnp.broadcast_to(row, decay_out_ref.shape[2:]))
            fresh_ref[site] = env_ref[site].astype(jnp.float32)
            for slot in range(slot_count):
                source = jnp.clip(src_ref[site, slot], 0, sector_count - 1)
                target = jnp.clip(dst_ref[site, slot], 0, sector_count - 1)
                above = jnp.where(first_ref[0] > 0, top_ref[site, source], recv_ref[site, source])
                product = jnp.dot(blocks_ref[site, slot], above, preferred_element_type=jnp.float32)
                fresh_ref[site, target] += jnp.where(slot < cnt_ref[site], product, 0.0)

    smem = pl.BlockSpec(memory_space=pltpu.SMEM)
    vmem = pl.BlockSpec(memory_space=pltpu.VMEM)
    return pl.pallas_call(
        body,
        in_specs=[smem] * 4 + [vmem] * 5,
        out_specs=(vmem, vmem),
        out_shape=(
            jax.ShapeDtypeStruct(environment.shape, jnp.float32),
            jax.ShapeDtypeStruct(environment.shape, jnp.float32),
        ),
    )(sources, targets, counts, first, blocks, top_env, received_env, environment, decays)


def backward_kernel(blocks, top_env, received_env, rounded, first, sources, targets, counts):
    site_count, slot_count = blocks.shape[:2]
    sector_count = top_env.shape[1]

    def body(src_ref, dst_ref, cnt_ref, first_ref, blocks_ref, top_ref, recv_ref, rounded_ref, grads_ref, ret_ref, acc_ref):
        for site in range(site_count):
            acc_ref[...] = jnp.zeros(acc_ref.shape, jnp.float32)
            for slot in range(slot_count):
                source = jnp.clip(src_ref[site, slot], 0, sector_count - 1)
                target = jnp.clip(dst_ref[site, slot], 0, sector_count - 1)
                live = slot < cnt_ref[site]
                picked = rounded_ref[site, target].astype(jnp.bfloat16)
                gathered = jnp.where(first_ref[0] > 0, top_ref[site, source], recv_ref[site, source])
                grad = lax.dot_general(
                    picked, gathered, (((1,), (1,)), ((), ())), preferred_element_type=jnp.float32
                )
                grads_ref[site, slot] = jnp.where(live, grad, 0.0).astype(grads_ref.dtype)
                contrib = lax.dot_general(
                    blocks_ref[site, slot], picked, (((0,), (0,)), ((), ())),
                    preferred_element_type=jnp.float32,
                )
                acc_ref[source] += jnp.where(live, contrib, 0.0)

            ret_ref[site] = acc_ref[...].astype(ret_ref.dtype)

    smem = pl.BlockSpec(memory_space=pltpu.SMEM)
    vmem = pl.BlockSpec(memory_space=pltpu.VMEM)
    return pl.pallas_call(
        body,
        in_specs=[smem] * 4 + [vmem] * 4,
        out_specs=(vmem, vmem),
        out_shape=(
            jax.ShapeDtypeStruct(blocks.shape, jnp.bfloat16),
            jax.ShapeDtypeStruct(top_env.shape, jnp.bfloat16),
        ),
        scratch_shapes=[pltpu.VMEM(top_env.shape[1:], jnp.float32)],
    )(sources, targets, counts, first, blocks, top_env, received_env, rounded)


def carry_kernel(got, part):
    count, _, channel_count = got.shape

    def body(got_ref, out_ref):
        diagonal = lax.broadcasted_iota(jnp.int32, (part, channel_count), 0) == lax.broadcasted_iota(
            jnp.int32, (part, channel_count), 1
        )
        factors = []
        for source in range(count):
            row = got_ref[source, pl.ds(2 * part, 1), :]
            factors.append(jnp.sum(jnp.where(diagonal, row, 0.0), axis=-1, keepdims=True))
        state = jnp.zeros((part, channel_count), jnp.float32)
        for source in range(count):
            out_ref[source, pl.ds(0, part), :] = state
            state = factors[source] * state + got_ref[source, pl.ds(0, part), :]
        state = jnp.zeros((part, channel_count), jnp.float32)
        for source in reversed(range(count)):
            out_ref[source, pl.ds(part, part), :] = state
            state = factors[source] * state + got_ref[source, pl.ds(part, part), :]

    return pl.pallas_call(
        body,
        out_shape=jax.ShapeDtypeStruct((count, 2 * part, channel_count), jnp.float32),
    )(got)


def summary_kernel(fresh, cotangent, decay_col, factor_row, count):
    col_count, rows, channel_count = fresh.shape
    part = rows // count

    def body(fresh_ref, weight_ref, decay_ref, factor_ref, out_ref):
        for chunk in range(count):
            span = pl.ds(chunk * part, part)
            state = fresh_ref[0, span, :]
            for column in range(1, col_count):
                state = decay_ref[column, span, :] * state + fresh_ref[column, span, :]
            grad = weight_ref[col_count - 1, span, :]
            for column in reversed(range(col_count - 1)):
                grad = weight_ref[column, span, :] + decay_ref[column + 1, span, :] * grad
            grad = decay_ref[0, span, :] * grad
            out_ref[chunk, pl.ds(0, part), :] = state
            out_ref[chunk, pl.ds(part, part), :] = grad
            out_ref[chunk, pl.ds(2 * part, 1), :] = factor_ref[pl.ds(chunk, 1), :]

    return pl.pallas_call(
        body,
        out_shape=jax.ShapeDtypeStruct((count, 2 * part + 1, channel_count), jnp.float32),
    )(fresh, cotangent, decay_col, factor_row)


def fixup_kernel(fresh, cotangent, decay_full, carries):
    col_count, rows, channel_count = fresh.shape
    count = carries.shape[0]
    part = rows // count

    def body(fresh_ref, weight_ref, decay_ref, carry_ref, grad_ref, prod_ref):
        for chunk in range(count):
            span = pl.ds(chunk * part, part)
            grad = carry_ref[chunk, pl.ds(part, part), :]
            grads = [None] * col_count
            for column in reversed(range(col_count)):
                grad = weight_ref[column, span, :] + grad
                grads[column] = grad
                grad_ref[column, span, :] = grad
                grad = decay_ref[column, span, :] * grad
            state = carry_ref[chunk, pl.ds(0, part), :]
            for column in range(col_count):
                prod_ref[column, span, :] = grads[column] * state
                state = decay_ref[column, span, :] * state + fresh_ref[column, span, :]

    grads, prods = pl.pallas_call(
        body,
        out_shape=(jax.ShapeDtypeStruct((col_count, rows, channel_count), jnp.float32),) * 2,
    )(fresh, cotangent, decay_full, carries)
    return (grads, jnp.sum(prods, -1))


def chain_scan(fresh, decay_rows, decay_full, cotangent):
    row_count, col_count, flat_rows, channel_count = fresh.shape
    count = lax.axis_size("col")
    rows = row_count * flat_rows
    part = rows // count
    assert part * count == rows and part <= channel_count

    def by_column(value):
        return jnp.swapaxes(value, 0, 1).reshape(col_count, rows, -1)

    fresh_c = by_column(fresh)
    weight_c = by_column(cotangent)
    decay_c = by_column(decay_full)
    factor = jnp.prod(jnp.swapaxes(decay_rows, 0, 1).reshape(col_count, count, part), 0)
    factor_row = jnp.pad(factor, ((0, 0), (0, channel_count - part)))
    payload = summary_kernel(fresh_c, weight_c, decay_c, factor_row, count)
    got = lax.all_to_all(payload, "col", 0, 0, tiled=True)
    carries = carry_kernel(got, part)
    ret = lax.all_to_all(carries, "col", 0, 0, tiled=True)
    grads, gates = fixup_kernel(fresh_c, weight_c, decay_c, ret)
    grads = jnp.swapaxes(grads.reshape(col_count, row_count, flat_rows, channel_count), 0, 1)
    gates = jnp.swapaxes(gates.reshape(col_count, row_count, flat_rows), 0, 1)
    return (grads, gates)


def local(blocks, sources, targets, counts, environment, top_boundary, decays, weights):
    row_count, col_count, sector_count, block_rows, channel_count = environment.shape
    flat_rows = sector_count * block_rows
    bottom = environment[row_count - 1]
    upper_env = from_behind(bottom, "row", 1)
    received_env = jnp.concatenate([upper_env[None], environment[: row_count - 1]], 0)
    top_env = jnp.concatenate([top_boundary[None], environment[: row_count - 1]], 0)
    first = (lax.axis_index("row") == 0).astype(jnp.int32).reshape(1)
    site_count = row_count * col_count

    def by_site(value):
        return value.reshape((site_count,) + value.shape[2:])

    fresh, decay_full = forward_kernel(
        by_site(blocks),
        by_site(top_env),
        by_site(received_env),
        by_site(environment),
        by_site(decays),
        first,
        sources.reshape(site_count, -1),
        targets.reshape(site_count, -1),
        counts.reshape(-1),
    )
    fresh = fresh.reshape(row_count, col_count, flat_rows, channel_count)
    decay_full = decay_full.reshape(row_count, col_count, flat_rows, channel_count)
    decay_rows = decays.reshape(row_count, col_count, flat_rows)
    cotangent = weights.reshape(row_count, col_count, flat_rows, channel_count)
    condition_derivative, gate_grad = chain_scan(fresh, decay_rows, decay_full, cotangent)
    condition_derivative = condition_derivative.reshape(environment.shape)
    grad_blocks, returned = backward_kernel(
        by_site(blocks),
        by_site(top_env),
        by_site(received_env),
        by_site(condition_derivative),
        first,
        sources.reshape(site_count, -1),
        targets.reshape(site_count, -1),
        counts.reshape(-1),
    )
    grad_blocks = grad_blocks.reshape(blocks.shape)
    returned = returned.reshape(environment.shape)
    below_rows = from_behind(returned[0], "row", -1)
    following_horizontals = jnp.concatenate([returned[1:], below_rows[None]], 0)
    grad_env = (condition_derivative + following_horizontals.astype(jnp.float32)).astype(
        jnp.bfloat16
    )
    grad_decays = gate_grad.reshape(decays.shape)
    return (grad_blocks, grad_env, grad_decays)


def solution(mesh):
    in_specs = (
        P("row", "col", None, None, None),
        P("row", "col", None),
        P("row", "col", None),
        P("row", "col"),
        P("row", "col", None, None, None),
        P("col", None, None, None),
        P("row", "col", None, None),
        P("row", "col", None, None, None),
    )
    out_specs = (
        P("row", "col", None, None, None),
        P("row", "col", None, None, None),
        P("row", "col", None, None),
    )
    return jax.shard_map(local, mesh=mesh, in_specs=in_specs, out_specs=out_specs, check_vma=False)
```

```python
import jax
import jax.numpy as jnp
from jax import lax
from jax.sharding import PartitionSpec as P
from jax.experimental import pallas as pl
from jax.experimental.pallas import tpu as pltpu


def from_behind(value, axis, steps):
    count = lax.axis_size(axis)
    initial, last = (max(0, -steps), min(count, count - steps))
    return lax.ppermute(value, axis, [(source, source + steps) for source in range(initial, last)])


def forward_kernel(blocks, top_env, received_env, environment, decays, first, sources, targets, counts):
    site_count, slot_count = blocks.shape[:2]
    sector_count = environment.shape[1]

    def body(
        src_ref, dst_ref, cnt_ref, first_ref, blocks_ref, top_ref, recv_ref, env_ref, decay_ref,
        fresh_ref, decay_out_ref,
    ):
        for site in range(site_count):
            for sector in range(sector_count):
                row = decay_ref[site, pl.ds(sector, 1), :]
                decay_out_ref[site, sector] = jnp.transpose(jnp.broadcast_to(row, decay_out_ref.shape[2:]))
            fresh_ref[site] = env_ref[site].astype(jnp.float32)
            for slot in range(slot_count):
                source = jnp.clip(src_ref[site, slot], 0, sector_count - 1)
                target = jnp.clip(dst_ref[site, slot], 0, sector_count - 1)
                above = jnp.where(first_ref[0] > 0, top_ref[site, source], recv_ref[site, source])
                product = jnp.dot(blocks_ref[site, slot], above, preferred_element_type=jnp.float32)
                fresh_ref[site, target] += jnp.where(slot < cnt_ref[site], product, 0.0)

    smem = pl.BlockSpec(memory_space=pltpu.SMEM)
    vmem = pl.BlockSpec(memory_space=pltpu.VMEM)
    return pl.pallas_call(
        body,
        in_specs=[smem] * 4 + [vmem] * 5,
        out_specs=(vmem, vmem),
        out_shape=(
            jax.ShapeDtypeStruct(environment.shape, jnp.float32),
            jax.ShapeDtypeStruct(environment.shape, jnp.float32),
        ),
    )(sources, targets, counts, first, blocks, top_env, received_env, environment, decays)


def backward_kernel(blocks, top_env, received_env, rounded, first, sources, targets, counts):
    site_count, slot_count = blocks.shape[:2]
    sector_count = top_env.shape[1]

    def body(src_ref, dst_ref, cnt_ref, first_ref, blocks_ref, top_ref, recv_ref, rounded_ref, grads_ref, ret_ref, acc_ref):
        for site in range(site_count):
            acc_ref[...] = jnp.zeros(acc_ref.shape, jnp.float32)
            for slot in range(slot_count):
                source = jnp.clip(src_ref[site, slot], 0, sector_count - 1)
                target = jnp.clip(dst_ref[site, slot], 0, sector_count - 1)
                live = slot < cnt_ref[site]
                picked = rounded_ref[site, target].astype(jnp.bfloat16)
                gathered = jnp.where(first_ref[0] > 0, top_ref[site, source], recv_ref[site, source])
                grad = lax.dot_general(
                    picked, gathered, (((1,), (1,)), ((), ())), preferred_element_type=jnp.float32
                )
                grads_ref[site, slot] = jnp.where(live, grad, 0.0).astype(grads_ref.dtype)
                contrib = lax.dot_general(
                    blocks_ref[site, slot], picked, (((0,), (0,)), ((), ())),
                    preferred_element_type=jnp.float32,
                )
                acc_ref[source] += jnp.where(live, contrib, 0.0)

            ret_ref[site] = acc_ref[...].astype(ret_ref.dtype)

    smem = pl.BlockSpec(memory_space=pltpu.SMEM)
    vmem = pl.BlockSpec(memory_space=pltpu.VMEM)
    return pl.pallas_call(
        body,
        in_specs=[smem] * 4 + [vmem] * 4,
        out_specs=(vmem, vmem),
        out_shape=(
            jax.ShapeDtypeStruct(blocks.shape, jnp.bfloat16),
            jax.ShapeDtypeStruct(top_env.shape, jnp.bfloat16),
        ),
        scratch_shapes=[pltpu.VMEM(top_env.shape[1:], jnp.float32)],
    )(sources, targets, counts, first, blocks, top_env, received_env, rounded)


def carry_kernel(got, part):
    count, _, channel_count = got.shape

    def body(got_ref, out_ref):
        diagonal = lax.broadcasted_iota(jnp.int32, (part, channel_count), 0) == lax.broadcasted_iota(
            jnp.int32, (part, channel_count), 1
        )
        factors = []
        for source in range(count):
            row = got_ref[source, pl.ds(2 * part, 1), :]
            factors.append(jnp.sum(jnp.where(diagonal, row, 0.0), axis=-1, keepdims=True))
        state = jnp.zeros((part, channel_count), jnp.float32)
        for source in range(count):
            out_ref[source, pl.ds(0, part), :] = state
            state = factors[source] * state + got_ref[source, pl.ds(0, part), :]
        state = jnp.zeros((part, channel_count), jnp.float32)
        for source in reversed(range(count)):
            out_ref[source, pl.ds(part, part), :] = state
            state = factors[source] * state + got_ref[source, pl.ds(part, part), :]

    return pl.pallas_call(
        body,
        out_shape=jax.ShapeDtypeStruct((count, 2 * part, channel_count), jnp.float32),
    )(got)


def summary_kernel(fresh, cotangent, decay_col, count):
    col_count, rows, channel_count = fresh.shape
    part = rows // count

    def body(fresh_ref, weight_ref, decay_ref, out_ref):
        diagonal = lax.broadcasted_iota(jnp.int32, (part, channel_count), 0) == lax.broadcasted_iota(
            jnp.int32, (part, channel_count), 1
        )
        for chunk in range(count):
            span = pl.ds(chunk * part, part)
            state = fresh_ref[0, span, :]
            for column in range(1, col_count):
                state = decay_ref[column, span, :] * state + fresh_ref[column, span, :]
            grad = weight_ref[col_count - 1, span, :]
            for column in reversed(range(col_count - 1)):
                grad = weight_ref[column, span, :] + decay_ref[column + 1, span, :] * grad
            grad = decay_ref[0, span, :] * grad
            out_ref[chunk, pl.ds(0, part), :] = state
            out_ref[chunk, pl.ds(part, part), :] = grad
            factor = decay_ref[0, span, :]
            for column in range(1, col_count):
                factor = factor * decay_ref[column, span, :]
            out_ref[chunk, pl.ds(2 * part, 1), :] = jnp.sum(
                jnp.where(diagonal, factor, 0.0), axis=0, keepdims=True
            )

    return pl.pallas_call(
        body,
        out_shape=jax.ShapeDtypeStruct((count, 2 * part + 1, channel_count), jnp.float32),
    )(fresh, cotangent, decay_col)


def fixup_kernel(fresh, cotangent, decay_full, carries):
    col_count, rows, channel_count = fresh.shape
    count = carries.shape[0]
    part = rows // count

    def body(fresh_ref, weight_ref, decay_ref, carry_ref, grad_ref, prod_ref):
        for chunk in range(count):
            span = pl.ds(chunk * part, part)
            grad = carry_ref[chunk, pl.ds(part, part), :]
            grads = [None] * col_count
            for column in reversed(range(col_count)):
                grad = weight_ref[column, span, :] + grad
                grads[column] = grad
                grad_ref[column, span, :] = grad
                grad = decay_ref[column, span, :] * grad
            state = carry_ref[chunk, pl.ds(0, part), :]
            for column in range(col_count):
                prod_ref[column, span, :] = grads[column] * state
                state = decay_ref[column, span, :] * state + fresh_ref[column, span, :]

    grads, prods = pl.pallas_call(
        body,
        out_shape=(jax.ShapeDtypeStruct((col_count, rows, channel_count), jnp.float32),) * 2,
    )(fresh, cotangent, decay_full, carries)
    return (grads, jnp.sum(prods, -1))


def chain_scan(fresh, decay_rows, decay_full, cotangent):
    row_count, col_count, flat_rows, channel_count = fresh.shape
    count = lax.axis_size("col")
    rows = row_count * flat_rows
    part = rows // count
    assert part * count == rows and part <= channel_count

    def by_column(value):
        return jnp.swapaxes(value, 0, 1).reshape(col_count, rows, -1)

    fresh_c = by_column(fresh)
    weight_c = by_column(cotangent)
    decay_c = by_column(decay_full)
    payload = summary_kernel(fresh_c, weight_c, decay_c, count)
    got = lax.all_to_all(payload, "col", 0, 0, tiled=True)
    carries = carry_kernel(got, part)
    ret = lax.all_to_all(carries, "col", 0, 0, tiled=True)
    grads, gates = fixup_kernel(fresh_c, weight_c, decay_c, ret)
    grads = jnp.swapaxes(grads.reshape(col_count, row_count, flat_rows, channel_count), 0, 1)
    gates = jnp.swapaxes(gates.reshape(col_count, row_count, flat_rows), 0, 1)
    return (grads, gates)


def local(blocks, sources, targets, counts, environment, top_boundary, decays, weights):
    row_count, col_count, sector_count, block_rows, channel_count = environment.shape
    flat_rows = sector_count * block_rows
    bottom = environment[row_count - 1]
    upper_env = from_behind(bottom, "row", 1)
    received_env = jnp.concatenate([upper_env[None], environment[: row_count - 1]], 0)
    top_env = jnp.concatenate([top_boundary[None], environment[: row_count - 1]], 0)
    first = (lax.axis_index("row") == 0).astype(jnp.int32).reshape(1)
    site_count = row_count * col_count

    def by_site(value):
        return value.reshape((site_count,) + value.shape[2:])

    fresh, decay_full = forward_kernel(
        by_site(blocks),
        by_site(top_env),
        by_site(received_env),
        by_site(environment),
        by_site(decays),
        first,
        sources.reshape(site_count, -1),
        targets.reshape(site_count, -1),
        counts.reshape(-1),
    )
    fresh = fresh.reshape(row_count, col_count, flat_rows, channel_count)
    decay_full = decay_full.reshape(row_count, col_count, flat_rows, channel_count)
    decay_rows = decays.reshape(row_count, col_count, flat_rows)
    cotangent = weights.reshape(row_count, col_count, flat_rows, channel_count)
    condition_derivative, gate_grad = chain_scan(fresh, decay_rows, decay_full, cotangent)
    condition_derivative = condition_derivative.reshape(environment.shape)
    grad_blocks, returned = backward_kernel(
        by_site(blocks),
        by_site(top_env),
        by_site(received_env),
        by_site(condition_derivative),
        first,
        sources.reshape(site_count, -1),
        targets.reshape(site_count, -1),
        counts.reshape(-1),
    )
    grad_blocks = grad_blocks.reshape(blocks.shape)
    returned = returned.reshape(environment.shape)
    below_rows = from_behind(returned[0], "row", -1)
    following_horizontals = jnp.concatenate([returned[1:], below_rows[None]], 0)
    grad_env = (condition_derivative + following_horizontals.astype(jnp.float32)).astype(
        jnp.bfloat16
    )
    grad_decays = gate_grad.reshape(decays.shape)
    return (grad_blocks, grad_env, grad_decays)


def solution(mesh):
    in_specs = (
        P("row", "col", None, None, None),
        P("row", "col", None),
        P("row", "col", None),
        P("row", "col"),
        P("row", "col", None, None, None),
        P("col", None, None, None),
        P("row", "col", None, None),
        P("row", "col", None, None, None),
    )
    out_specs = (
        P("row", "col", None, None, None),
        P("row", "col", None, None, None),
        P("row", "col", None, None),
    )
    return jax.shard_map(local, mesh=mesh, in_specs=in_specs, out_specs=out_specs, check_vma=False)
```

```python
import jax
import jax.numpy as jnp
from jax import lax
from jax.sharding import PartitionSpec as P
from jax.experimental import pallas as pl
from jax.experimental.pallas import tpu as pltpu


def from_behind(value, axis, steps):
    count = lax.axis_size(axis)
    initial, last = (max(0, -steps), min(count, count - steps))
    return lax.ppermute(value, axis, [(source, source + steps) for source in range(initial, last)])


def forward_kernel(blocks, top_env, received_env, environment, decays, first, sources, targets, counts):
    site_count, slot_count = blocks.shape[:2]
    sector_count = environment.shape[1]

    def body(
        src_ref, dst_ref, cnt_ref, first_ref, blocks_ref, top_ref, recv_ref, env_ref, decay_ref,
        fresh_ref, decay_out_ref,
    ):
        for site in range(site_count):
            for sector in range(sector_count):
                row = decay_ref[site, pl.ds(sector, 1), :]
                decay_out_ref[site, sector] = jnp.transpose(jnp.broadcast_to(row, decay_out_ref.shape[2:]))
            fresh_ref[site] = env_ref[site].astype(jnp.float32)
            for slot in range(slot_count):
                source = jnp.clip(src_ref[site, slot], 0, sector_count - 1)
                target = jnp.clip(dst_ref[site, slot], 0, sector_count - 1)
                above = jnp.where(first_ref[0] > 0, top_ref[site, source], recv_ref[site, source])
                product = jnp.dot(blocks_ref[site, slot], above, preferred_element_type=jnp.float32)
                fresh_ref[site, target] += jnp.where(slot < cnt_ref[site], product, 0.0)

    smem = pl.BlockSpec(memory_space=pltpu.SMEM)
    vmem = pl.BlockSpec(memory_space=pltpu.VMEM)
    return pl.pallas_call(
        body,
        in_specs=[smem] * 4 + [vmem] * 5,
        out_specs=(vmem, vmem),
        out_shape=(
            jax.ShapeDtypeStruct(environment.shape, jnp.float32),
            jax.ShapeDtypeStruct(environment.shape, jnp.float32),
        ),
    )(sources, targets, counts, first, blocks, top_env, received_env, environment, decays)


def backward_kernel(blocks, top_env, received_env, rounded, first, sources, targets, counts, want_returned):
    site_count, slot_count = blocks.shape[:2]
    sector_count = top_env.shape[1]

    def body(src_ref, dst_ref, cnt_ref, first_ref, blocks_ref, top_ref, recv_ref, rounded_ref, out_ref, *scratch):
        for site in range(site_count):
            if want_returned:
                scratch[0][...] = jnp.zeros(scratch[0].shape, jnp.float32)
            for slot in range(slot_count):
                source = jnp.clip(src_ref[site, slot], 0, sector_count - 1)
                target = jnp.clip(dst_ref[site, slot], 0, sector_count - 1)
                live = slot < cnt_ref[site]
                picked = rounded_ref[site, target].astype(jnp.bfloat16)
                if want_returned:
                    contrib = lax.dot_general(
                        blocks_ref[site, slot], picked, (((0,), (0,)), ((), ())),
                        preferred_element_type=jnp.float32,
                    )
                    scratch[0][source] += jnp.where(live, contrib, 0.0)
                else:
                    gathered = jnp.where(first_ref[0] > 0, top_ref[site, source], recv_ref[site, source])
                    grad = lax.dot_general(
                        picked, gathered, (((1,), (1,)), ((), ())), preferred_element_type=jnp.float32
                    )
                    out_ref[site, slot] = jnp.where(live, grad, 0.0).astype(out_ref.dtype)
            if want_returned:
                out_ref[site] = scratch[0][...].astype(out_ref.dtype)

    smem = pl.BlockSpec(memory_space=pltpu.SMEM)
    vmem = pl.BlockSpec(memory_space=pltpu.VMEM)
    shape = top_env.shape if want_returned else blocks.shape
    return pl.pallas_call(
        body,
        in_specs=[smem] * 4 + [vmem] * 4,
        out_specs=vmem,
        out_shape=jax.ShapeDtypeStruct(shape, jnp.bfloat16),
        scratch_shapes=[pltpu.VMEM(top_env.shape[1:], jnp.float32)] if want_returned else [],
    )(sources, targets, counts, first, blocks, top_env, received_env, rounded)


def carry_kernel(got, part):
    count, _, channel_count = got.shape

    def body(got_ref, out_ref):
        diagonal = lax.broadcasted_iota(jnp.int32, (part, channel_count), 0) == lax.broadcasted_iota(
            jnp.int32, (part, channel_count), 1
        )
        factors = []
        for source in range(count):
            row = got_ref[source, pl.ds(2 * part, 1), :]
            factors.append(jnp.sum(jnp.where(diagonal, row, 0.0), axis=-1, keepdims=True))
        state = jnp.zeros((part, channel_count), jnp.float32)
        for source in range(count):
            out_ref[source, pl.ds(0, part), :] = state
            state = factors[source] * state + got_ref[source, pl.ds(0, part), :]
        state = jnp.zeros((part, channel_count), jnp.float32)
        for source in reversed(range(count)):
            out_ref[source, pl.ds(part, part), :] = state
            state = factors[source] * state + got_ref[source, pl.ds(part, part), :]

    return pl.pallas_call(
        body,
        out_shape=jax.ShapeDtypeStruct((count, 2 * part, channel_count), jnp.float32),
    )(got)


def summary_kernel(fresh, cotangent, decay_col, count):
    col_count, rows, channel_count = fresh.shape
    part = rows // count

    def body(fresh_ref, weight_ref, decay_ref, out_ref):
        diagonal = lax.broadcasted_iota(jnp.int32, (part, channel_count), 0) == lax.broadcasted_iota(
            jnp.int32, (part, channel_count), 1
        )
        for chunk in range(count):
            span = pl.ds(chunk * part, part)
            state = fresh_ref[0, span, :]
            for column in range(1, col_count):
                state = decay_ref[column, span, :] * state + fresh_ref[column, span, :]
            grad = weight_ref[col_count - 1, span, :]
            for column in reversed(range(col_count - 1)):
                grad = weight_ref[column, span, :] + decay_ref[column + 1, span, :] * grad
            grad = decay_ref[0, span, :] * grad
            out_ref[chunk, pl.ds(0, part), :] = state
            out_ref[chunk, pl.ds(part, part), :] = grad
            factor = decay_ref[0, span, :]
            for column in range(1, col_count):
                factor = factor * decay_ref[column, span, :]
            out_ref[chunk, pl.ds(2 * part, 1), :] = jnp.sum(
                jnp.where(diagonal, factor, 0.0), axis=0, keepdims=True
            )

    return pl.pallas_call(
        body,
        out_shape=jax.ShapeDtypeStruct((count, 2 * part + 1, channel_count), jnp.float32),
    )(fresh, cotangent, decay_col)


def fixup_kernel(fresh, cotangent, decay_full, carries):
    col_count, rows, channel_count = fresh.shape
    count = carries.shape[0]
    part = rows // count

    def body(fresh_ref, weight_ref, decay_ref, carry_ref, grad_ref, prod_ref):
        for chunk in range(count):
            span = pl.ds(chunk * part, part)
            grad = carry_ref[chunk, pl.ds(part, part), :]
            grads = [None] * col_count
            for column in reversed(range(col_count)):
                grad = weight_ref[column, span, :] + grad
                grads[column] = grad
                grad_ref[column, span, :] = grad
                grad = decay_ref[column, span, :] * grad
            state = carry_ref[chunk, pl.ds(0, part), :]
            for column in range(col_count):
                prod_ref[column, span, :] = grads[column] * state
                state = decay_ref[column, span, :] * state + fresh_ref[column, span, :]

    grads, prods = pl.pallas_call(
        body,
        out_shape=(jax.ShapeDtypeStruct((col_count, rows, channel_count), jnp.float32),) * 2,
    )(fresh, cotangent, decay_full, carries)
    return (grads, jnp.sum(prods, -1))


def chain_scan(fresh, decay_rows, decay_full, cotangent):
    row_count, col_count, flat_rows, channel_count = fresh.shape
    count = lax.axis_size("col")
    rows = row_count * flat_rows
    part = rows // count
    assert part * count == rows and part <= channel_count

    def by_column(value):
        return jnp.swapaxes(value, 0, 1).reshape(col_count, rows, -1)

    fresh_c = by_column(fresh)
    weight_c = by_column(cotangent)
    decay_c = by_column(decay_full)
    payload = summary_kernel(fresh_c, weight_c, decay_c, count)
    got = lax.all_to_all(payload, "col", 0, 0, tiled=True)
    carries = carry_kernel(got, part)
    ret = lax.all_to_all(carries, "col", 0, 0, tiled=True)
    grads, gates = fixup_kernel(fresh_c, weight_c, decay_c, ret)
    grads = jnp.swapaxes(grads.reshape(col_count, row_count, flat_rows, channel_count), 0, 1)
    gates = jnp.swapaxes(gates.reshape(col_count, row_count, flat_rows), 0, 1)
    return (grads, gates)


def local(blocks, sources, targets, counts, environment, top_boundary, decays, weights):
    row_count, col_count, sector_count, block_rows, channel_count = environment.shape
    flat_rows = sector_count * block_rows
    bottom = environment[row_count - 1]
    upper_env = from_behind(bottom, "row", 1)
    received_env = jnp.concatenate([upper_env[None], environment[: row_count - 1]], 0)
    top_env = jnp.concatenate([top_boundary[None], environment[: row_count - 1]], 0)
    first = (lax.axis_index("row") == 0).astype(jnp.int32).reshape(1)
    site_count = row_count * col_count

    def by_site(value):
        return value.reshape((site_count,) + value.shape[2:])

    fresh, decay_full = forward_kernel(
        by_site(blocks),
        by_site(top_env),
        by_site(received_env),
        by_site(environment),
        by_site(decays),
        first,
        sources.reshape(site_count, -1),
        targets.reshape(site_count, -1),
        counts.reshape(-1),
    )
    fresh = fresh.reshape(row_count, col_count, flat_rows, channel_count)
    decay_full = decay_full.reshape(row_count, col_count, flat_rows, channel_count)
    decay_rows = decays.reshape(row_count, col_count, flat_rows)
    cotangent = weights.reshape(row_count, col_count, flat_rows, channel_count)
    condition_derivative, gate_grad = chain_scan(fresh, decay_rows, decay_full, cotangent)
    condition_derivative = condition_derivative.reshape(environment.shape)
    backward_args = (
        by_site(blocks),
        by_site(top_env),
        by_site(received_env),
        by_site(condition_derivative),
        first,
        sources.reshape(site_count, -1),
        targets.reshape(site_count, -1),
        counts.reshape(-1),
    )
    returned = backward_kernel(*backward_args, True)
    grad_blocks = backward_kernel(*backward_args, False)
    grad_blocks = grad_blocks.reshape(blocks.shape)
    returned = returned.reshape(environment.shape)
    below_rows = from_behind(returned[0], "row", -1)
    following_horizontals = jnp.concatenate([returned[1:], below_rows[None]], 0)
    grad_env = (condition_derivative + following_horizontals.astype(jnp.float32)).astype(
        jnp.bfloat16
    )
    grad_decays = gate_grad.reshape(decays.shape)
    return (grad_blocks, grad_env, grad_decays)


def solution(mesh):
    in_specs = (
        P("row", "col", None, None, None),
        P("row", "col", None),
        P("row", "col", None),
        P("row", "col"),
        P("row", "col", None, None, None),
        P("col", None, None, None),
        P("row", "col", None, None),
        P("row", "col", None, None, None),
    )
    out_specs = (
        P("row", "col", None, None, None),
        P("row", "col", None, None, None),
        P("row", "col", None, None),
    )
    return jax.shard_map(local, mesh=mesh, in_specs=in_specs, out_specs=out_specs, check_vma=False)
```

```python
import jax
import jax.numpy as jnp
from jax import lax
from jax.sharding import PartitionSpec as P
from jax.experimental import pallas as pl
from jax.experimental.pallas import tpu as pltpu


def from_behind(value, axis, steps):
    count = lax.axis_size(axis)
    initial, last = (max(0, -steps), min(count, count - steps))
    return lax.ppermute(value, axis, [(source, source + steps) for source in range(initial, last)])


def forward_kernel(blocks, top_env, received_env, environment, decays, first, sources, targets, counts):
    site_count, slot_count = blocks.shape[:2]
    sector_count = environment.shape[1]

    def body(
        src_ref, dst_ref, cnt_ref, first_ref, blocks_ref, top_ref, recv_ref, env_ref, decay_ref,
        fresh_ref, decay_out_ref,
    ):
        for site in range(site_count):
            for sector in range(sector_count):
                row = decay_ref[site, pl.ds(sector, 1), :]
                decay_out_ref[site, sector] = jnp.transpose(jnp.broadcast_to(row, decay_out_ref.shape[2:]))
            fresh_ref[site] = env_ref[site].astype(jnp.float32)
            for slot in range(slot_count):
                source = jnp.clip(src_ref[site, slot], 0, sector_count - 1)
                target = jnp.clip(dst_ref[site, slot], 0, sector_count - 1)
                above = jnp.where(first_ref[0] > 0, top_ref[site, source], recv_ref[site, source])
                product = jnp.dot(blocks_ref[site, slot], above, preferred_element_type=jnp.float32)
                fresh_ref[site, target] += jnp.where(slot < cnt_ref[site], product, 0.0)

    smem = pl.BlockSpec(memory_space=pltpu.SMEM)
    vmem = pl.BlockSpec(memory_space=pltpu.VMEM)
    return pl.pallas_call(
        body,
        in_specs=[smem] * 4 + [vmem] * 5,
        out_specs=(vmem, vmem),
        out_shape=(
            jax.ShapeDtypeStruct(environment.shape, jnp.float32),
            jax.ShapeDtypeStruct(environment.shape, jnp.float32),
        ),
    )(sources, targets, counts, first, blocks, top_env, received_env, environment, decays)


def backward_kernel(blocks, top_env, received_env, rounded, first, sources, targets, counts, want_returned):
    site_count, slot_count = blocks.shape[:2]
    sector_count = top_env.shape[1]

    def body(src_ref, dst_ref, cnt_ref, first_ref, blocks_ref, top_ref, recv_ref, rounded_ref, out_ref, *scratch):
        for site in range(site_count):
            if want_returned:
                scratch[0][...] = jnp.zeros(scratch[0].shape, jnp.float32)
            for slot in range(slot_count):
                source = jnp.clip(src_ref[site, slot], 0, sector_count - 1)
                target = jnp.clip(dst_ref[site, slot], 0, sector_count - 1)
                live = slot < cnt_ref[site]
                picked = rounded_ref[site, target].astype(jnp.bfloat16)
                if want_returned:
                    contrib = lax.dot_general(
                        blocks_ref[site, slot], picked, (((0,), (0,)), ((), ())),
                        preferred_element_type=jnp.float32,
                    )
                    scratch[0][source] += jnp.where(live, contrib, 0.0)
                else:
                    gathered = jnp.where(first_ref[0] > 0, top_ref[site, source], recv_ref[site, source])
                    grad = lax.dot_general(
                        picked, gathered, (((1,), (1,)), ((), ())), preferred_element_type=jnp.float32
                    )
                    out_ref[site, slot] = jnp.where(live, grad, 0.0).astype(out_ref.dtype)
            if want_returned:
                out_ref[site] = scratch[0][...].astype(out_ref.dtype)

    smem = pl.BlockSpec(memory_space=pltpu.SMEM)
    vmem = pl.BlockSpec(memory_space=pltpu.VMEM)
    shape = top_env.shape if want_returned else blocks.shape
    return pl.pallas_call(
        body,
        in_specs=[smem] * 4 + [vmem] * 4,
        out_specs=vmem,
        out_shape=jax.ShapeDtypeStruct(shape, jnp.bfloat16),
        scratch_shapes=[pltpu.VMEM(top_env.shape[1:], jnp.float32)] if want_returned else [],
    )(sources, targets, counts, first, blocks, top_env, received_env, rounded)


def carry_kernel(got, part):
    count, _, channel_count = got.shape

    def body(got_ref, out_ref):
        diagonal = lax.broadcasted_iota(jnp.int32, (part, channel_count), 0) == lax.broadcasted_iota(
            jnp.int32, (part, channel_count), 1
        )
        factors = []
        for source in range(count):
            row = got_ref[source, pl.ds(2 * part, 1), :]
            factors.append(jnp.sum(jnp.where(diagonal, row, 0.0), axis=-1, keepdims=True))
        state = jnp.zeros((part, channel_count), jnp.float32)
        for source in range(count):
            out_ref[source, pl.ds(0, part), :] = state
            state = factors[source] * state + got_ref[source, pl.ds(0, part), :]
        state = jnp.zeros((part, channel_count), jnp.float32)
        for source in reversed(range(count)):
            out_ref[source, pl.ds(part, part), :] = state
            state = factors[source] * state + got_ref[source, pl.ds(part, part), :]

    return pl.pallas_call(
        body,
        out_shape=jax.ShapeDtypeStruct((count, 2 * part, channel_count), jnp.float32),
    )(got)


def summary_kernel(fresh, cotangent, decay_col, count):
    col_count, rows, channel_count = fresh.shape
    part = rows // count

    def body(fresh_ref, weight_ref, decay_ref, out_ref):
        diagonal = lax.broadcasted_iota(jnp.int32, (part, channel_count), 0) == lax.broadcasted_iota(
            jnp.int32, (part, channel_count), 1
        )
        for chunk in range(count):
            span = pl.ds(chunk * part, part)
            state = fresh_ref[0, span, :]
            for column in range(1, col_count):
                state = decay_ref[column, span, :] * state + fresh_ref[column, span, :]
            grad = weight_ref[col_count - 1, span, :]
            for column in reversed(range(col_count - 1)):
                grad = weight_ref[column, span, :] + decay_ref[column + 1, span, :] * grad
            grad = decay_ref[0, span, :] * grad
            out_ref[chunk, pl.ds(0, part), :] = state
            out_ref[chunk, pl.ds(part, part), :] = grad
            factor = decay_ref[0, span, :]
            for column in range(1, col_count):
                factor = factor * decay_ref[column, span, :]
            out_ref[chunk, pl.ds(2 * part, 1), :] = jnp.sum(
                jnp.where(diagonal, factor, 0.0), axis=0, keepdims=True
            )

    return pl.pallas_call(
        body,
        out_shape=jax.ShapeDtypeStruct((count, 2 * part + 1, channel_count), jnp.float32),
    )(fresh, cotangent, decay_col)


def fixup_kernel(fresh, cotangent, decay_full, carries, want_products):
    col_count, rows, channel_count = fresh.shape
    count = carries.shape[0]
    part = rows // count

    def body(fresh_ref, weight_ref, decay_ref, carry_ref, out_ref):
        for chunk in range(count):
            span = pl.ds(chunk * part, part)
            grad = carry_ref[chunk, pl.ds(part, part), :]
            grads = [None] * col_count
            for column in reversed(range(col_count)):
                grad = weight_ref[column, span, :] + grad
                grads[column] = grad
                if not want_products:
                    out_ref[column, span, :] = grad
                grad = decay_ref[column, span, :] * grad
            if want_products:
                state = carry_ref[chunk, pl.ds(0, part), :]
                for column in range(col_count):
                    out_ref[column, span, :] = grads[column] * state
                    state = decay_ref[column, span, :] * state + fresh_ref[column, span, :]

    return pl.pallas_call(
        body,
        out_shape=jax.ShapeDtypeStruct((col_count, rows, channel_count), jnp.float32),
    )(fresh, cotangent, decay_full, carries)


def chain_scan(fresh, decay_rows, decay_full, cotangent):
    row_count, col_count, flat_rows, channel_count = fresh.shape
    count = lax.axis_size("col")
    rows = row_count * flat_rows
    part = rows // count
    assert part * count == rows and part <= channel_count

    def by_column(value):
        return jnp.swapaxes(value, 0, 1).reshape(col_count, rows, -1)

    fresh_c = by_column(fresh)
    weight_c = by_column(cotangent)
    decay_c = by_column(decay_full)
    payload = summary_kernel(fresh_c, weight_c, decay_c, count)
    got = lax.all_to_all(payload, "col", 0, 0, tiled=True)
    carries = carry_kernel(got, part)
    ret = lax.all_to_all(carries, "col", 0, 0, tiled=True)
    grads = fixup_kernel(fresh_c, weight_c, decay_c, ret, False)
    gates = jnp.sum(fixup_kernel(fresh_c, weight_c, decay_c, ret, True), -1)
    grads = jnp.swapaxes(grads.reshape(col_count, row_count, flat_rows, channel_count), 0, 1)
    gates = jnp.swapaxes(gates.reshape(col_count, row_count, flat_rows), 0, 1)
    return (grads, gates)


def local(blocks, sources, targets, counts, environment, top_boundary, decays, weights):
    row_count, col_count, sector_count, block_rows, channel_count = environment.shape
    flat_rows = sector_count * block_rows
    bottom = environment[row_count - 1]
    upper_env = from_behind(bottom, "row", 1)
    received_env = jnp.concatenate([upper_env[None], environment[: row_count - 1]], 0)
    top_env = jnp.concatenate([top_boundary[None], environment[: row_count - 1]], 0)
    first = (lax.axis_index("row") == 0).astype(jnp.int32).reshape(1)
    site_count = row_count * col_count

    def by_site(value):
        return value.reshape((site_count,) + value.shape[2:])

    fresh, decay_full = forward_kernel(
        by_site(blocks),
        by_site(top_env),
        by_site(received_env),
        by_site(environment),
        by_site(decays),
        first,
        sources.reshape(site_count, -1),
        targets.reshape(site_count, -1),
        counts.reshape(-1),
    )
    fresh = fresh.reshape(row_count, col_count, flat_rows, channel_count)
    decay_full = decay_full.reshape(row_count, col_count, flat_rows, channel_count)
    decay_rows = decays.reshape(row_count, col_count, flat_rows)
    cotangent = weights.reshape(row_count, col_count, flat_rows, channel_count)
    condition_derivative, gate_grad = chain_scan(fresh, decay_rows, decay_full, cotangent)
    condition_derivative = condition_derivative.reshape(environment.shape)
    backward_args = (
        by_site(blocks),
        by_site(top_env),
        by_site(received_env),
        by_site(condition_derivative),
        first,
        sources.reshape(site_count, -1),
        targets.reshape(site_count, -1),
        counts.reshape(-1),
    )
    returned = backward_kernel(*backward_args, True)
    grad_blocks = backward_kernel(*backward_args, False)
    grad_blocks = grad_blocks.reshape(blocks.shape)
    returned = returned.reshape(environment.shape)
    below_rows = from_behind(returned[0], "row", -1)
    following_horizontals = jnp.concatenate([returned[1:], below_rows[None]], 0)
    grad_env = (condition_derivative + following_horizontals.astype(jnp.float32)).astype(
        jnp.bfloat16
    )
    grad_decays = gate_grad.reshape(decays.shape)
    return (grad_blocks, grad_env, grad_decays)


def solution(mesh):
    in_specs = (
        P("row", "col", None, None, None),
        P("row", "col", None),
        P("row", "col", None),
        P("row", "col"),
        P("row", "col", None, None, None),
        P("col", None, None, None),
        P("row", "col", None, None),
        P("row", "col", None, None, None),
    )
    out_specs = (
        P("row", "col", None, None, None),
        P("row", "col", None, None, None),
        P("row", "col", None, None),
    )
    return jax.shard_map(local, mesh=mesh, in_specs=in_specs, out_specs=out_specs, check_vma=False)
```
